256 devices in a mesh: dp: 4 (over x), expert: 64 (over z, y, core).
Axes of the slice: x: 4, y: 4, z: 8, core: 2. Of those that a mesh axis runs over, the one named last changes fastest.
Arguments:
- hidden_in: bfloat16 [16384, 2048], P(('dp', 'expert')), may hold values from -6 to 6
- context: bfloat16 [16384, 2, 2048], P(('dp', 'expert')), may hold values from -6 to 6
- att_routes: int32 [16384, 2], P(('dp', 'expert')), may hold values from 0 to 7, all different within a row; in each aligned block of 64 rows (0 to 63, 64 to 127, ...) at most 20 rows name the same one
- att_logits: float32 [16384, 8], P(('dp', 'expert')), may hold values from -6 to 6
- ffn_routes: int32 [16384, 2], P(('dp', 'expert')), may hold values from 0 to 7, all different within a row; in each aligned block of 64 rows (0 to 63, 64 to 127, ...) at most 20 rows name the same one
- ffn_logits: float32 [16384, 8], P(('dp', 'expert')), may hold values from -6 to 6
- att_output_map: bfloat16 [64, 2048, 256], P('expert', 'dp'), may hold values from -0.125 to 0.125
- ffn_gate_up: bfloat16 [64, 2048, 2, 704], P('expert', 'dp'), may hold values from -0.125 to 0.125
- ffn_down: bfloat16 [64, 704, 2048], P('expert', None, 'dp'), may hold values from -0.078125 to 0.078125
- norm_gain: bfloat16 [2048], replicated, may hold values from 0.5 to 1.5
- out_gain: bfloat16 [2048], replicated, may hold values from 0.5 to 1.5
Outputs:
- layer_out: bfloat16 [16384, 2048], P(('dp', 'expert'))
The draws below stay inside these ranges and needn't reach their ends.
Inputs may be any that keep to these rules, and one draw needn't show every extreme that they name: `att_routes`: the two ids of a row differ. In the rows of one device no attention expert is named more than 20 times, and on some device one is named exactly 20 times. `ffn_routes`: the two ids of a row differ. In the rows of one device no feed-forward expert is named more than 20 times, and on some device one is named exactly 20 times.
All inputs are finite; a program needn't handle non-finite values.
Results may differ from the reference program's by a relative error of at most 0.0054.
Values may be sent and summed in bfloat16 or wider, within the bound.
No kernel may reach another device: no remote copies, remote signals or barrier semaphores. Data moves between devices by JAX's collectives and lax.ppermute only.
A program may use at most 128 MiB of HBM per device.

```python
import math
import jax
import jax.numpy as jnp
import numpy as np
from jax import lax

D = 2048
FF = 5632
EXPERTS = 8
ROWS = 64
ATT = 2048
S = 8
HID = 704
DS = 256
CAP = 20
TOKENS = 16384
N_DP = 4
N_EXPERT = 64


def level_of(rng, dims, pieces, least, largest):
    level, own = 1.0, jax.random.fold_in(rng, 6)
    for axis_at, shards_of in pieces:
        steps = jnp.exp(jax.random.uniform(jax.random.fold_in(own, axis_at), (shards_of,), jnp.float32, least / len(pieces), largest / len(pieces)))
        level = level * jnp.repeat(steps, dims[axis_at] // shards_of).reshape([-1 if axis == axis_at else 1 for axis in range(len(dims))])
    return level


def deal_out(rng, own, number, rows, number_of, top, limit, lean):
    order = jax.random.permutation(rng, number_of)
    packed, ordinary = portions_of(number_of, rows * top, limit, lean, True), portions_of(number_of, rows * top, limit, lean, False)
    places = jnp.arange(number_of)

    def named(tallies, turn):
        used = int((tallies > 0).sum())
        fixed = max(1, used // 4)
        moved = fixed + (places - fixed + turn * (used - fixed)) % max(1, number_of - fixed)
        return jnp.zeros((number_of,), jnp.int32).at[order[jnp.where(places < fixed, places, moved)]].set(jnp.asarray(tallies, jnp.int32))

    tallies = jnp.where(number % 4 == 0, named(packed, number // 4), named(ordinary, number - number // 4 - 1))
    mixed = jax.random.permutation(jax.random.fold_in(own, 3), number_of)
    source_of, taker = mixed[0:number_of // 2 * 2:2], mixed[1:number_of // 2 * 2:2]
    margin = jnp.minimum(tallies[source_of] - 1, limit - tallies[taker]) // 2
    margin = jnp.where((source_of == order[0]) | (taker == order[0]) | (tallies[taker] == 0), 0, jnp.maximum(margin, 0))
    moved = jax.random.randint(jax.random.fold_in(own, 4), (number_of // 2,), 0, 1 << 20) % (margin + 1)
    tallies = tallies.at[source_of].add(-moved).at[taker].add(moved)
    members = jnp.searchsorted(jnp.cumsum(tallies), jnp.arange(rows * top), side="right").astype(jnp.int32)
    grid = members.reshape(top, rows).T
    grid = grid[jax.random.permutation(jax.random.fold_in(own, 1), rows)]
    turn = jax.random.randint(jax.random.fold_in(own, 2), (rows, 1), 0, top)
    return jnp.take_along_axis(grid, (jnp.arange(top)[None, :] + turn) % top, axis=1)


def portions_of(number_of, total, limit, skew, full):
    loads = [(1 << 20) // math.isqrt(grade ** skew) + 1 for grade in range(1, number_of + 1)]
    largest = limit if full else min(limit, max(-(-total // number_of), total * loads[0] // sum(loads)))
    least = 1 if total - largest >= number_of - 1 else 0
    counts, rest = [largest] + [least] * (number_of - 1), total - largest - least * (number_of - 1)
    while rest > 0:
        free = [i for i in range(1, number_of) if counts[i] < largest] or [i for i in range(1, number_of) if counts[i] < limit]
        whole, remaining = sum([loads[i] for i in free]), rest
        for i in free:
            more = min(limit - counts[i], max(1, remaining * loads[i] // whole), rest)
            counts[i] = counts[i] + more
            rest = rest - more
    return np.array(counts)


def gaussian(key, extent, width, bound, split=(), kind=jnp.bfloat16):
    level = level_of(key, extent, split, -0.22, 0.18) if split else 1.0
    values = jax.random.normal(key, extent, jnp.float32) * width * level
    return jnp.minimum(jnp.maximum(values, -bound), bound).astype(kind)


def setup_inputs(seed: int = 0) -> dict:
    splits = jax.random.split(jax.random.key(seed), 12)
    hidden_in = gaussian(splits[0], (TOKENS, D), 1.0, 6.0, ((0, 256),))
    context = gaussian(splits[1], (TOKENS, 2, ATT), 1.0, 6.0, ((0, 256),))
    att_routes_keys = jax.random.split(jax.random.fold_in(splits[2], 1), TOKENS // ROWS)
    att_routes_turns = jax.random.permutation(jax.random.fold_in(splits[2], 3), TOKENS // ROWS)
    att_routes = jax.vmap(lambda own, number: deal_out(jax.random.fold_in(splits[2], 2), own, number, ROWS, EXPERTS, 2, CAP, 1))(att_routes_keys, att_routes_turns).reshape((TOKENS, 2))
    att_logits = gaussian(splits[3], (TOKENS, EXPERTS), 1.0, 6.0, ((0, 256),), jnp.float32)
    ffn_routes_keys = jax.random.split(jax.random.fold_in(splits[4], 1), TOKENS // ROWS)
    ffn_routes_turns = jax.random.permutation(jax.random.fold_in(splits[4], 3), TOKENS // ROWS)
    ffn_routes = jax.vmap(lambda own, number: deal_out(jax.random.fold_in(splits[4], 2), own, number, ROWS, EXPERTS, 2, CAP, 1))(ffn_routes_keys, ffn_routes_turns).reshape((TOKENS, 2))
    ffn_logits = gaussian(splits[5], (TOKENS, EXPERTS), 1.0, 6.0, ((0, 256),), jnp.float32)
    att_output_map = gaussian(splits[6], (EXPERTS * S, ATT, DS), ATT ** -0.5, 0.125, ((0, 64), (1, 4)))
    ffn_gate_up = gaussian(splits[7], (EXPERTS * S, D, 2, HID), D ** -0.5, 0.125, ((0, 64), (1, 4)))
    ffn_down = gaussian(splits[8], (EXPERTS * S, HID, D), FF ** -0.5, 0.078125, ((0, 64), (2, 4)))
    norm_gain = jnp.clip(1.0 + 0.1 * jax.random.normal(splits[9], (D,), jnp.float32), 0.5, 1.5).astype(jnp.bfloat16)
    out_gain = jnp.clip(1.0 + 0.1 * jax.random.normal(splits[10], (D,), jnp.float32), 0.5, 1.5).astype(jnp.bfloat16)
    return {"hidden_in": hidden_in, "context": context, "att_routes": att_routes, "att_logits": att_logits, "ffn_routes": ffn_routes, "ffn_logits": ffn_logits, "att_output_map": att_output_map, "ffn_gate_up": ffn_gate_up, "ffn_down": ffn_down, "norm_gain": norm_gain, "out_gain": out_gain}


EPSILON = 1e-06

def norm_rows(values, gain):
    mean_square = lax.optimization_barrier(jnp.mean(values * values, axis=-1, keepdims=True))
    return values * lax.rsqrt(mean_square + EPSILON) * gain.astype(jnp.float32)

def pair_weights(logits, routes):
    chosen = jnp.take_along_axis(logits, routes, axis=1)
    first_weight = jax.nn.sigmoid(chosen[:, 0] - chosen[:, 1])
    return jnp.stack([first_weight, 1.0 - first_weight], axis=1)

def routed_rows(route_list, expert, capacity):
    row_total = route_list.shape[0]
    positions = jnp.arange(row_total, dtype=jnp.int32)
    sort_keys = jnp.where(route_list == expert, positions, row_total)
    picked = jnp.argsort(sort_keys, stable=True)[:capacity].astype(jnp.int32)
    is_live = route_list[picked] == expert
    return (picked, is_live)

def rounded(values):
    return lax.optimization_barrier(values.astype(jnp.bfloat16)).astype(jnp.float32)

def reference(hidden_in, context, att_routes, att_logits, ffn_routes, ffn_logits, att_output_map, ffn_gate_up, ffn_down, norm_gain, out_gain):
    row_total = hidden_in.shape[0]
    capacity = CAP * N_DP * N_EXPERT
    att_list = att_routes.reshape(-1)
    context_rows = context.reshape(row_total * 2, ATT)
    maps_all = att_output_map.reshape(EXPERTS, S, ATT, DS)
    mapped = jnp.zeros((row_total * 2, D), jnp.float32)
    for expert in range(EXPERTS):
        picked, is_live = routed_rows(att_list, expert, capacity)
        matrix = jnp.transpose(maps_all[expert], (1, 0, 2)).reshape(ATT, D)
        result = rounded(jnp.dot(context_rows[picked], matrix, preferred_element_type=jnp.float32))
        mapped = mapped.at[picked].add(jnp.where(is_live[:, None], result, 0.0))
    mapped = mapped.reshape(row_total, 2, D)
    att_weight = pair_weights(att_logits, att_routes)
    hidden_state = hidden_in.astype(jnp.float32) + att_weight[:, 0:1] * mapped[:, 0] + att_weight[:, 1:2] * mapped[:, 1]
    ffn_in = norm_rows(hidden_state, norm_gain).astype(jnp.bfloat16)
    ffn_list = ffn_routes.reshape(-1)
    gate_all = ffn_gate_up.reshape(EXPERTS, S, D, 2, HID)
    down_all = ffn_down.reshape(EXPERTS, S, HID, D)
    expert_out = jnp.zeros((row_total * 2, D), jnp.float32)
    for expert in range(EXPERTS):
        picked, is_live = routed_rows(ffn_list, expert, capacity)
        matrix = jnp.transpose(gate_all[expert], (1, 2, 0, 3)).reshape(D, 2 * FF)
        gate_up = jnp.dot(ffn_in[picked // 2], matrix, preferred_element_type=jnp.float32).reshape(-1, 2, FF)
        expert_hidden = (jax.nn.silu(gate_up[:, 0]) * gate_up[:, 1]).astype(jnp.bfloat16)
        running = jnp.zeros((capacity, D), jnp.float32)
        for slice_index in range(S):
            columns = expert_hidden[:, slice_index * HID:(slice_index + 1) * HID]
            running = running + rounded(jnp.dot(columns, down_all[expert, slice_index], preferred_element_type=jnp.float32))
        expert_out = expert_out.at[picked].add(jnp.where(is_live[:, None], running, 0.0))
    expert_out = expert_out.reshape(row_total, 2, D)
    ffn_weight = pair_weights(ffn_logits, ffn_routes)
    mixed_sum = hidden_state + (ffn_weight[:, 0:1] * expert_out[:, 0] + ffn_weight[:, 1:2] * expert_out[:, 1])
    return norm_rows(mixed_sum, out_gain).astype(jnp.bfloat16)
```

```python
import jax
import jax.numpy as jnp
import numpy as np
from jax import lax
from jax.sharding import Mesh
from jax.sharding import PartitionSpec as P

EXPERTS = 8
CAP = 20


EPSILON = 1e-06


def norm_rows(values, gain):
    mean_square = jnp.mean(values * values, axis=-1, keepdims=True)
    return values * lax.rsqrt(mean_square + EPSILON) * gain.astype(jnp.float32)


def pair_weights(logits, routes):
    expert_ids = jnp.arange(logits.shape[1], dtype=jnp.int32)
    selected = routes[:, :, None] == expert_ids[None, None, :]
    chosen = jnp.sum(jnp.where(selected, logits[:, None, :], 0.0), axis=2)
    first_weight = jax.nn.sigmoid(chosen[:, 0] - chosen[:, 1])
    return jnp.stack([first_weight, 1.0 - first_weight], axis=1)


def slot_matrix(routes, capacity, experts):
    route_list = routes.reshape(-1)
    onehot = (route_list[:, None] == jnp.arange(experts, dtype=jnp.int32)[None, :]).astype(
        jnp.int32
    )
    before = jnp.cumsum(onehot, axis=0) - onehot
    slot_index = jnp.sum(before * onehot, axis=1)
    target = route_list * capacity + slot_index
    slot_ids = jnp.arange(experts * capacity, dtype=jnp.int32)
    return slot_ids[:, None] == target[None, :]


def dispatch(blocks):
    arrived = lax.all_to_all(blocks, "ez", split_axis=0, concat_axis=0, tiled=True)
    n_eh = lax.axis_size("eh")
    copies = jnp.broadcast_to(arrived[None], (n_eh,) + arrived.shape)
    return lax.all_to_all(copies, "eh", split_axis=0, concat_axis=0, tiled=True)


def local(
    hidden_in,
    context,
    att_routes,
    att_logits,
    ffn_routes,
    ffn_logits,
    att_output_map,
    ffn_gate_up,
    ffn_down,
    norm_gain,
    out_gain,
):
    rows_dev = hidden_in.shape[0]
    model_width = hidden_in.shape[1]
    att_dim = context.shape[2]
    out_slice = att_output_map.shape[2]
    hid_slice = ffn_gate_up.shape[3]
    n_ez = lax.axis_size("ez")
    n_eh = lax.axis_size("eh")
    capacity = CAP

    att_matrix = lax.all_gather(att_output_map, "dp", axis=1, tiled=True)[0]
    gate_matrix = lax.all_gather(ffn_gate_up, "dp", axis=1, tiled=True)[0]
    down_matrix = lax.all_gather(ffn_down, "dp", axis=2, tiled=True)[0]

    att_weight = pair_weights(att_logits, att_routes)
    att_place = slot_matrix(att_routes, capacity, EXPERTS)
    outgoing = jnp.dot(
        att_place.astype(jnp.bfloat16),
        context.reshape(-1, att_dim),
        preferred_element_type=jnp.float32,
    ).astype(jnp.bfloat16)
    incoming = dispatch(outgoing.reshape(EXPERTS, capacity, att_dim))
    mapped = jnp.dot(
        incoming.reshape(-1, att_dim), att_matrix, preferred_element_type=jnp.float32
    ).astype(jnp.bfloat16)
    mapped = mapped.reshape(n_eh, n_ez, capacity, out_slice)
    mapped = jnp.transpose(mapped, (1, 0, 2, 3)).reshape(n_ez * n_eh, capacity, out_slice)
    back = lax.all_to_all(mapped, ("ez", "eh"), split_axis=0, concat_axis=0, tiled=True)
    back = back.reshape(EXPERTS, n_eh, capacity, out_slice)
    back = jnp.transpose(back, (0, 2, 1, 3)).reshape(EXPERTS * capacity, model_width)
    picked = jnp.dot(
        att_place.T.astype(jnp.bfloat16), back, preferred_element_type=jnp.float32
    )
    picked = picked.reshape(rows_dev, 2, model_width)
    hidden_state = (
        hidden_in.astype(jnp.float32)
        + att_weight[:, 0:1] * picked[:, 0]
        + att_weight[:, 1:2] * picked[:, 1]
    )
    ffn_in = norm_rows(hidden_state, norm_gain).astype(jnp.bfloat16)
    ffn_place = slot_matrix(ffn_routes, capacity, EXPERTS)
    row_place = jnp.any(ffn_place.reshape(EXPERTS * capacity, rows_dev, 2), axis=2)
    outgoing_rows = jnp.dot(
        row_place.astype(jnp.bfloat16), ffn_in, preferred_element_type=jnp.float32
    ).astype(jnp.bfloat16)
    incoming = dispatch(outgoing_rows.reshape(EXPERTS, capacity, model_width))
    flattened = incoming.reshape(-1, model_width)
    depth = gate_matrix.shape[0]
    gate_up = jnp.dot(
        flattened, gate_matrix.reshape(depth, 2 * hid_slice), preferred_element_type=jnp.float32
    )
    gate_up = gate_up.reshape(-1, 2, hid_slice)
    activated = (jax.nn.silu(gate_up[:, 0]) * gate_up[:, 1]).astype(jnp.bfloat16)
    projected = jnp.dot(
        activated, down_matrix, preferred_element_type=jnp.float32
    ).astype(jnp.bfloat16)
    projected = projected.reshape(n_eh, n_ez, capacity, model_width)
    reduced = lax.psum_scatter(projected, "eh", scatter_dimension=0, tiled=True)[0]
    summed = lax.all_to_all(reduced, "ez", split_axis=0, concat_axis=0, tiled=True)
    summed = summed.reshape(EXPERTS * capacity, model_width).astype(jnp.float32)
    ffn_weight = pair_weights(ffn_logits, ffn_routes)
    weighted = ffn_place.astype(jnp.float32) * ffn_weight.reshape(1, -1)
    expert_mix = jnp.dot(weighted.T, summed, precision=lax.Precision.HIGHEST).reshape(
        rows_dev, 2, model_width
    )
    mixed_sum = hidden_state + (expert_mix[:, 0] + expert_mix[:, 1])
    return norm_rows(mixed_sum, out_gain).astype(jnp.bfloat16)


def solution(mesh):
    n_dp = mesh.devices.shape[0]
    n_expert = mesh.devices.shape[1]
    grid = Mesh(
        mesh.devices.reshape(n_dp, EXPERTS, n_expert // EXPERTS), ("dp", "ez", "eh")
    )
    rows = ("dp", "ez", "eh")
    owners = ("ez", "eh")
    return jax.shard_map(
        local,
        mesh=grid,
        in_specs=(
            P(rows, None),
            P(rows, None, None),
            P(rows, None),
            P(rows, None),
            P(rows, None),
            P(rows, None),
            P(owners, "dp", None),
            P(owners, "dp", None, None),
            P(owners, None, "dp"),
            P(),
            P(),
        ),
        out_specs=P(rows, None),
        check_vma=False,
    )
```

```python
import jax
import jax.numpy as jnp
from jax import lax
from jax.sharding import Mesh
from jax.sharding import PartitionSpec as P

EXPERTS = 8
CAP = 20
CORES = 2


EPSILON = 1e-06


def norm_rows(values, gain):
    mean_square = jnp.mean(values * values, axis=-1, keepdims=True)
    return values * lax.rsqrt(mean_square + EPSILON) * gain.astype(jnp.float32)


def pair_weights(logits, routes):
    expert_ids = jnp.arange(logits.shape[1], dtype=jnp.int32)
    selected = routes[:, :, None] == expert_ids[None, None, :]
    chosen = jnp.sum(jnp.where(selected, logits[:, None, :], 0.0), axis=2)
    first_weight = jax.nn.sigmoid(chosen[:, 0] - chosen[:, 1])
    return jnp.stack([first_weight, 1.0 - first_weight], axis=1)


def slot_matrix(routes, capacity, experts):
    route_list = routes.reshape(-1)
    onehot = (route_list[:, None] == jnp.arange(experts, dtype=jnp.int32)[None, :]).astype(
        jnp.int32
    )
    before = jnp.cumsum(onehot, axis=0) - onehot
    slot_index = jnp.sum(before * onehot, axis=1)
    target = slot_index * experts + route_list
    slot_ids = jnp.arange(experts * capacity, dtype=jnp.int32)
    return slot_ids[:, None] == target[None, :]


def dispatch(blocks):
    arrived = lax.all_to_all(blocks, "ez", split_axis=1, concat_axis=1, tiled=True)
    n_ey = lax.axis_size("ey")
    copies = jnp.broadcast_to(arrived[None], (n_ey,) + arrived.shape)
    across = lax.all_to_all(copies, "ey", split_axis=0, concat_axis=0, tiled=True)
    pair = jnp.broadcast_to(across[None], (CORES,) + across.shape)
    return lax.all_to_all(pair, "ec", split_axis=0, concat_axis=0, tiled=True)


def local(
    hidden_in,
    context,
    att_routes,
    att_logits,
    ffn_routes,
    ffn_logits,
    att_output_map,
    ffn_gate_up,
    ffn_down,
    norm_gain,
    out_gain,
):
    rows_dev = hidden_in.shape[0]
    model_width = hidden_in.shape[1]
    att_dim = context.shape[2]
    out_slice = att_output_map.shape[2]
    hid_slice = ffn_gate_up.shape[3]
    n_ez = lax.axis_size("ez")
    n_ey = lax.axis_size("ey")
    capacity = CAP

    att_matrix = lax.all_gather(att_output_map, "dp", axis=1, tiled=True)[0]
    gate_matrix = lax.all_gather(ffn_gate_up, "dp", axis=1, tiled=True)[0]
    down_matrix = lax.all_gather(ffn_down, "dp", axis=2, tiled=True)[0]

    att_weight = pair_weights(att_logits, att_routes)
    att_place = slot_matrix(att_routes, capacity, EXPERTS)
    outgoing = jnp.dot(
        att_place.astype(jnp.bfloat16),
        context.reshape(-1, att_dim),
        preferred_element_type=jnp.float32,
    ).astype(jnp.bfloat16)
    incoming = dispatch(outgoing.reshape(capacity, EXPERTS, att_dim))
    mapped = jnp.dot(
        incoming.reshape(-1, att_dim), att_matrix, preferred_element_type=jnp.float32
    ).astype(jnp.bfloat16)
    mapped = mapped.reshape(CORES, n_ey, capacity, n_ez, out_slice)
    mapped = jnp.transpose(mapped, (3, 1, 0, 2, 4)).reshape(
        n_ez * n_ey * CORES, capacity, out_slice
    )
    back = lax.all_to_all(mapped, ("ez", "ey", "ec"), split_axis=0, concat_axis=0, tiled=True)
    back = back.reshape(EXPERTS, n_ey * CORES, capacity, out_slice)
    back = jnp.transpose(back, (2, 0, 1, 3)).reshape(capacity * EXPERTS, model_width)
    picked = jnp.dot(
        att_place.T.astype(jnp.bfloat16), back, preferred_element_type=jnp.float32
    )
    picked = picked.reshape(rows_dev, 2, model_width)
    hidden_state = (
        hidden_in.astype(jnp.float32)
        + att_weight[:, 0:1] * picked[:, 0]
        + att_weight[:, 1:2] * picked[:, 1]
    )
    ffn_in = norm_rows(hidden_state, norm_gain).astype(jnp.bfloat16)
    ffn_place = slot_matrix(ffn_routes, capacity, EXPERTS)
    row_place = jnp.any(ffn_place.reshape(EXPERTS * capacity, rows_dev, 2), axis=2)
    outgoing_rows = jnp.dot(
        row_place.astype(jnp.bfloat16), ffn_in, preferred_element_type=jnp.float32
    ).astype(jnp.bfloat16)
    incoming = dispatch(outgoing_rows.reshape(capacity, EXPERTS, model_width))
    flattened = incoming.reshape(-1, model_width)
    depth = gate_matrix.shape[0]
    gate_up = jnp.dot(
        flattened, gate_matrix.reshape(depth, 2 * hid_slice), preferred_element_type=jnp.float32
    )
    gate_up = gate_up.reshape(-1, 2, hid_slice)
    activated = (jax.nn.silu(gate_up[:, 0]) * gate_up[:, 1]).astype(jnp.bfloat16)
    projected = jnp.dot(
        activated, down_matrix, preferred_element_type=jnp.float32
    ).astype(jnp.bfloat16)
    projected = projected.reshape(CORES * n_ey, capacity * n_ez, model_width)
    reduced = lax.psum_scatter(projected, ("ec", "ey"), scatter_dimension=0, tiled=True)[0]
    reduced = reduced.reshape(capacity, n_ez, model_width)
    summed = lax.all_to_all(reduced, "ez", split_axis=1, concat_axis=1, tiled=True)
    summed = summed.reshape(capacity * EXPERTS, model_width).astype(jnp.float32)
    ffn_weight = pair_weights(ffn_logits, ffn_routes)
    weighted = ffn_place.astype(jnp.float32) * ffn_weight.reshape(1, -1)
    expert_mix = jnp.dot(weighted.T, summed, precision=lax.Precision.HIGHEST).reshape(
        rows_dev, 2, model_width
    )
    mixed_sum = hidden_state + (expert_mix[:, 0] + expert_mix[:, 1])
    return norm_rows(mixed_sum, out_gain).astype(jnp.bfloat16)


def solution(mesh):
    n_dp = mesh.devices.shape[0]
    n_expert = mesh.devices.shape[1]
    n_ey = n_expert // (EXPERTS * CORES)
    grid = Mesh(
        mesh.devices.reshape(n_dp, EXPERTS, n_ey, CORES), ("dp", "ez", "ey", "ec")
    )
    rows = ("dp", "ez", "ey", "ec")
    owners = ("ez", "ey", "ec")
    return jax.shard_map(
        local,
        mesh=grid,
        in_specs=(
            P(rows, None),
            P(rows, None, None),
            P(rows, None),
            P(rows, None),
            P(rows, None),
            P(rows, None),
            P(owners, "dp", None),
            P(owners, "dp", None, None),
            P(owners, None, "dp"),
            P(),
            P(),
        ),
        out_specs=P(rows, None),
        check_vma=False,
    )
```

```python
import jax
import jax.numpy as jnp
from jax import lax
from jax.sharding import Mesh
from jax.sharding import PartitionSpec as P

EXPERTS = 8
CAP = 20
CORES = 2


EPSILON = 1e-06


def norm_rows(values, gain):
    mean_square = jnp.mean(values * values, axis=-1, keepdims=True)
    return values * lax.rsqrt(mean_square + EPSILON) * gain.astype(jnp.float32)


def pair_weights(logits, routes):
    expert_ids = jnp.arange(logits.shape[1], dtype=jnp.int32)
    selected = routes[:, :, None] == expert_ids[None, None, :]
    chosen = jnp.sum(jnp.where(selected, logits[:, None, :], 0.0), axis=2)
    first_weight = jax.nn.sigmoid(chosen[:, 0] - chosen[:, 1])
    return jnp.stack([first_weight, 1.0 - first_weight], axis=1)


def slot_matrix(routes, capacity, experts):
    route_list = routes.reshape(-1)
    onehot = (route_list[:, None] == jnp.arange(experts, dtype=jnp.int32)[None, :]).astype(
        jnp.int32
    )
    before = jnp.cumsum(onehot, axis=0) - onehot
    slot_index = jnp.sum(before * onehot, axis=1)
    target = slot_index * experts + route_list
    slot_ids = jnp.arange(experts * capacity, dtype=jnp.int32)
    return slot_ids[:, None] == target[None, :]


def dispatch(blocks):
    arrived = lax.all_to_all(blocks, "ez", split_axis=1, concat_axis=1, tiled=True)
    n_ey = lax.axis_size("ey")
    copies = jnp.broadcast_to(arrived[None], (n_ey,) + arrived.shape)
    across = lax.all_to_all(copies, "ey", split_axis=0, concat_axis=0, tiled=True)
    pair = jnp.broadcast_to(across[None], (CORES,) + across.shape)
    return lax.all_to_all(pair, "ec", split_axis=0, concat_axis=0, tiled=True)


def local(
    hidden_in,
    context,
    att_routes,
    att_logits,
    ffn_routes,
    ffn_logits,
    att_output_map,
    ffn_gate_up,
    ffn_down,
    norm_gain,
    out_gain,
):
    rows_dev = hidden_in.shape[0]
    model_width = hidden_in.shape[1]
    att_dim = context.shape[2]
    out_slice = att_output_map.shape[2]
    hid_slice = ffn_gate_up.shape[3]
    n_ez = lax.axis_size("ez")
    n_ey = lax.axis_size("ey")
    capacity = CAP

    att_matrix = lax.all_gather(att_output_map, "dp", axis=1, tiled=True)[0]
    gate_matrix = lax.all_gather(ffn_gate_up, "dp", axis=1, tiled=True)[0]
    down_matrix = lax.all_gather(ffn_down, "dp", axis=2, tiled=True)[0]

    att_weight = pair_weights(att_logits, att_routes)
    att_place = slot_matrix(att_routes, capacity, EXPERTS)
    outgoing = jnp.dot(
        att_place.astype(jnp.bfloat16),
        context.reshape(-1, att_dim),
        preferred_element_type=jnp.float32,
    ).astype(jnp.bfloat16)
    incoming = dispatch(outgoing.reshape(capacity, EXPERTS, att_dim))
    mapped = jnp.dot(
        incoming.reshape(-1, att_dim), att_matrix, preferred_element_type=jnp.float32
    ).astype(jnp.bfloat16)
    mapped = mapped.reshape(CORES, n_ey, capacity, n_ez, out_slice)
    mapped = jnp.transpose(mapped, (3, 1, 0, 2, 4)).reshape(
        n_ez * n_ey * CORES, capacity, out_slice
    )
    back = lax.all_to_all(mapped, ("ez", "ey", "ec"), split_axis=0, concat_axis=0, tiled=True)
    back = back.reshape(EXPERTS, n_ey * CORES, capacity, out_slice)
    back = jnp.transpose(back, (2, 0, 1, 3)).reshape(capacity * EXPERTS, model_width)
    picked = jnp.dot(
        att_place.T.astype(jnp.bfloat16), back, preferred_element_type=jnp.float32
    )
    picked = picked.reshape(rows_dev, 2, model_width)
    hidden_state = (
        hidden_in.astype(jnp.float32)
        + att_weight[:, 0:1] * picked[:, 0]
        + att_weight[:, 1:2] * picked[:, 1]
    )
    ffn_in = norm_rows(hidden_state, norm_gain).astype(jnp.bfloat16)
    ffn_place = slot_matrix(ffn_routes, capacity, EXPERTS)
    row_place = jnp.any(ffn_place.reshape(EXPERTS * capacity, rows_dev, 2), axis=2)
    outgoing_rows = jnp.dot(
        row_place.astype(jnp.bfloat16), ffn_in, preferred_element_type=jnp.float32
    ).astype(jnp.bfloat16)
    incoming = dispatch(outgoing_rows.reshape(capacity, EXPERTS, model_width))
    flattened = incoming.reshape(-1, model_width)
    depth = gate_matrix.shape[0]
    gate_up = jnp.dot(
        flattened, gate_matrix.reshape(depth, 2 * hid_slice), preferred_element_type=jnp.float32
    )
    gate_up = gate_up.reshape(-1, 2, hid_slice)
    activated = (jax.nn.silu(gate_up[:, 0]) * gate_up[:, 1]).astype(jnp.bfloat16)
    projected = jnp.dot(
        activated, down_matrix, preferred_element_type=jnp.float32
    ).astype(jnp.bfloat16)
    projected = projected.reshape(CORES, n_ey * capacity * n_ez, model_width)
    reduced = lax.psum_scatter(projected, "ec", scatter_dimension=0, tiled=True)[0]
    reduced = reduced.reshape(n_ey, capacity * n_ez, model_width)
    reduced = lax.psum_scatter(reduced, "ey", scatter_dimension=0, tiled=True)[0]
    reduced = reduced.reshape(capacity, n_ez, model_width)
    summed = lax.all_to_all(reduced, "ez", split_axis=1, concat_axis=1, tiled=True)
    summed = summed.reshape(capacity * EXPERTS, model_width).astype(jnp.float32)
    ffn_weight = pair_weights(ffn_logits, ffn_routes)
    weighted = ffn_place.astype(jnp.float32) * ffn_weight.reshape(1, -1)
    expert_mix = jnp.dot(weighted.T, summed, precision=lax.Precision.HIGHEST).reshape(
        rows_dev, 2, model_width
    )
    mixed_sum = hidden_state + (expert_mix[:, 0] + expert_mix[:, 1])
    return norm_rows(mixed_sum, out_gain).astype(jnp.bfloat16)


def solution(mesh):
    n_dp = mesh.devices.shape[0]
    n_expert = mesh.devices.shape[1]
    n_ey = n_expert // (EXPERTS * CORES)
    grid = Mesh(
        mesh.devices.reshape(n_dp, EXPERTS, n_ey, CORES), ("dp", "ez", "ey", "ec")
    )
    rows = ("dp", "ez", "ey", "ec")
    owners = ("ez", "ey", "ec")
    return jax.shard_map(
        local,
        mesh=grid,
        in_specs=(
            P(rows, None),
            P(rows, None, None),
            P(rows, None),
            P(rows, None),
            P(rows, None),
            P(rows, None),
            P(owners, "dp", None),
            P(owners, "dp", None, None),
            P(owners, None, "dp"),
            P(),
            P(),
        ),
        out_specs=P(rows, None),
        check_vma=False,
    )
```

```python
import jax
import jax.numpy as jnp
from jax import lax
from jax.sharding import Mesh
from jax.sharding import PartitionSpec as P

EXPERTS = 8
CAP = 20
CORES = 2


EPSILON = 1e-06


def norm_rows(values, gain):
    mean_square = jnp.mean(values * values, axis=-1, keepdims=True)
    return values * lax.rsqrt(mean_square + EPSILON) * gain.astype(jnp.float32)


def pair_weights(logits, routes):
    expert_ids = jnp.arange(logits.shape[1], dtype=jnp.int32)
    selected = routes[:, :, None] == expert_ids[None, None, :]
    chosen = jnp.sum(jnp.where(selected, logits[:, None, :], 0.0), axis=2)
    first_weight = jax.nn.sigmoid(chosen[:, 0] - chosen[:, 1])
    return jnp.stack([first_weight, 1.0 - first_weight], axis=1)


def slot_matrix(routes, capacity, experts):
    route_list = routes.reshape(-1)
    onehot = (route_list[:, None] == jnp.arange(experts, dtype=jnp.int32)[None, :]).astype(
        jnp.int32
    )
    before = jnp.cumsum(onehot, axis=0) - onehot
    slot_index = jnp.sum(before * onehot, axis=1)
    target = slot_index * experts + route_list
    slot_ids = jnp.arange(experts * capacity, dtype=jnp.int32)
    return slot_ids[:, None] == target[None, :]


def dispatch(blocks):
    n_ey = lax.axis_size("ey")
    copies = jnp.broadcast_to(blocks[:, :, None], blocks.shape[:2] + (n_ey,) + blocks.shape[2:])
    copies = copies.reshape(blocks.shape[0], -1, blocks.shape[2])
    arrived = lax.all_to_all(copies, ("ez", "ey"), split_axis=1, concat_axis=1, tiled=True)
    pair = jnp.broadcast_to(arrived[None], (CORES,) + arrived.shape)
    return lax.all_to_all(pair, "ec", split_axis=0, concat_axis=0, tiled=True)


def local(
    hidden_in,
    context,
    att_routes,
    att_logits,
    ffn_routes,
    ffn_logits,
    att_output_map,
    ffn_gate_up,
    ffn_down,
    norm_gain,
    out_gain,
):
    rows_dev = hidden_in.shape[0]
    model_width = hidden_in.shape[1]
    att_dim = context.shape[2]
    out_slice = att_output_map.shape[2]
    hid_slice = ffn_gate_up.shape[3]
    n_ez = lax.axis_size("ez")
    n_ey = lax.axis_size("ey")
    capacity = CAP

    att_matrix = lax.all_gather(att_output_map, "dp", axis=1, tiled=True)[0]
    gate_matrix = lax.all_gather(ffn_gate_up, "dp", axis=1, tiled=True)[0]
    down_matrix = lax.all_gather(ffn_down, "dp", axis=2, tiled=True)[0]

    att_weight = pair_weights(att_logits, att_routes)
    att_place = slot_matrix(att_routes, capacity, EXPERTS)
    outgoing = jnp.dot(
        att_place.astype(jnp.bfloat16),
        context.reshape(-1, att_dim),
        preferred_element_type=jnp.float32,
    ).astype(jnp.bfloat16)
    incoming = dispatch(outgoing.reshape(capacity, EXPERTS, att_dim))
    mapped = jnp.dot(
        incoming.reshape(-1, att_dim), att_matrix, preferred_element_type=jnp.float32
    ).astype(jnp.bfloat16)
    mapped = mapped.reshape(CORES, capacity, n_ez, n_ey, out_slice)
    mapped = jnp.transpose(mapped, (2, 3, 0, 1, 4)).reshape(
        n_ez * n_ey * CORES, capacity, out_slice
    )
    back = lax.all_to_all(mapped, ("ez", "ey", "ec"), split_axis=0, concat_axis=0, tiled=True)
    back = back.reshape(EXPERTS, n_ey * CORES, capacity, out_slice)
    back = jnp.transpose(back, (2, 0, 1, 3)).reshape(capacity * EXPERTS, model_width)
    picked = jnp.dot(
        att_place.T.astype(jnp.bfloat16), back, preferred_element_type=jnp.float32
    )
    picked = picked.reshape(rows_dev, 2, model_width)
    hidden_state = (
        hidden_in.astype(jnp.float32)
        + att_weight[:, 0:1] * picked[:, 0]
        + att_weight[:, 1:2] * picked[:, 1]
    )
    ffn_in = norm_rows(hidden_state, norm_gain).astype(jnp.bfloat16)
    ffn_place = slot_matrix(ffn_routes, capacity, EXPERTS)
    row_place = jnp.any(ffn_place.reshape(EXPERTS * capacity, rows_dev, 2), axis=2)
    outgoing_rows = jnp.dot(
        row_place.astype(jnp.bfloat16), ffn_in, preferred_element_type=jnp.float32
    ).astype(jnp.bfloat16)
    incoming = dispatch(outgoing_rows.reshape(capacity, EXPERTS, model_width))
    flattened = incoming.reshape(-1, model_width)
    depth = gate_matrix.shape[0]
    gate_up = jnp.dot(
        flattened, gate_matrix.reshape(depth, 2 * hid_slice), preferred_element_type=jnp.float32
    )
    gate_up = gate_up.reshape(-1, 2, hid_slice)
    activated = (jax.nn.silu(gate_up[:, 0]) * gate_up[:, 1]).astype(jnp.bfloat16)
    projected = jnp.dot(
        activated, down_matrix, preferred_element_type=jnp.float32
    ).astype(jnp.bfloat16)
    projected = projected.reshape(CORES, capacity * n_ez * n_ey, model_width)
    reduced = lax.psum_scatter(projected, "ec", scatter_dimension=0, tiled=True)[0]
    reduced = reduced.reshape(capacity, n_ez * n_ey, model_width)
    parts = lax.all_to_all(reduced, ("ez", "ey"), split_axis=1, concat_axis=1, tiled=True)
    parts = parts.reshape(capacity, EXPERTS, n_ey, model_width).astype(jnp.float32)
    summed = jnp.sum(parts, axis=2).reshape(capacity * EXPERTS, model_width)
    ffn_weight = pair_weights(ffn_logits, ffn_routes)
    weighted = ffn_place.astype(jnp.float32) * ffn_weight.reshape(1, -1)
    expert_mix = jnp.dot(weighted.T, summed, precision=lax.Precision.HIGHEST).reshape(
        rows_dev, 2, model_width
    )
    mixed_sum = hidden_state + (expert_mix[:, 0] + expert_mix[:, 1])
    return norm_rows(mixed_sum, out_gain).astype(jnp.bfloat16)


def solution(mesh):
    n_dp = mesh.devices.shape[0]
    n_expert = mesh.devices.shape[1]
    n_ey = n_expert // (EXPERTS * CORES)
    grid = Mesh(
        mesh.devices.reshape(n_dp, EXPERTS, n_ey, CORES), ("dp", "ez", "ey", "ec")
    )
    rows = ("dp", "ez", "ey", "ec")
    owners = ("ez", "ey", "ec")
    return jax.shard_map(
        local,
        mesh=grid,
        in_specs=(
            P(rows, None),
            P(rows, None, None),
            P(rows, None),
            P(rows, None),
            P(rows, None),
            P(rows, None),
            P(owners, "dp", None),
            P(owners, "dp", None, None),
            P(owners, None, "dp"),
            P(),
            P(),
        ),
        out_specs=P(rows, None),
        check_vma=False,
    )
```

```python
import jax
import jax.numpy as jnp
from jax import lax
from jax.sharding import Mesh
from jax.sharding import PartitionSpec as P

EXPERTS = 8
CAP = 20
CORES = 2


EPSILON = 1e-06


def norm_rows(values, gain):
    mean_square = jnp.mean(values * values, axis=-1, keepdims=True)
    return values * lax.rsqrt(mean_square + EPSILON) * gain.astype(jnp.float32)


def pair_weights(logits, routes):
    expert_ids = jnp.arange(logits.shape[1], dtype=jnp.int32)
    selected = routes[:, :, None] == expert_ids[None, None, :]
    chosen = jnp.sum(jnp.where(selected, logits[:, None, :], 0.0), axis=2)
    first_weight = jax.nn.sigmoid(chosen[:, 0] - chosen[:, 1])
    return jnp.stack([first_weight, 1.0 - first_weight], axis=1)


def slot_matrix(routes, capacity, experts):
    route_list = routes.reshape(-1)
    onehot = (route_list[:, None] == jnp.arange(experts, dtype=jnp.int32)[None, :]).astype(
        jnp.int32
    )
    before = jnp.cumsum(onehot, axis=0) - onehot
    slot_index = jnp.sum(before * onehot, axis=1)
    target = slot_index * experts + route_list
    slot_ids = jnp.arange(experts * capacity, dtype=jnp.int32)
    return slot_ids[:, None] == target[None, :]


def from_left(x):
    n = lax.axis_size("ey")
    return lax.ppermute(x, "ey", [(i, (i + 1) % n) for i in range(n)])


def from_right(x):
    n = lax.axis_size("ey")
    return lax.ppermute(x, "ey", [(i, (i - 1) % n) for i in range(n)])


def ring_copies(block):
    half = block.shape[0] // 2
    left = from_left(block)
    right = from_right(block)
    far = jnp.concatenate([from_left(left[:half]), from_right(right[half:])], axis=0)
    return jnp.stack([block, right, far, left], axis=0)


def ring_sums(parts):
    half = parts.shape[1] // 2
    far = parts[2].astype(jnp.bfloat16)
    early_right = from_right(far[:half]).astype(jnp.float32)
    early_left = from_left(far[half:]).astype(jnp.float32)
    to_left = jnp.concatenate([parts[3, :half] + early_right, parts[3, half:]], axis=0)
    to_right = jnp.concatenate([parts[1, :half], parts[1, half:] + early_left], axis=0)
    got_right = from_right(to_left.astype(jnp.bfloat16)).astype(jnp.float32)
    got_left = from_left(to_right.astype(jnp.bfloat16)).astype(jnp.float32)
    return parts[0] + got_right + got_left


def dispatch(blocks):
    arrived = lax.all_to_all(blocks, "ez", split_axis=1, concat_axis=1, tiled=True)
    across = ring_copies(arrived)
    pair = jnp.broadcast_to(across[None], (CORES,) + across.shape)
    return lax.all_to_all(pair, "ec", split_axis=0, concat_axis=0, tiled=True)


def local(
    hidden_in,
    context,
    att_routes,
    att_logits,
    ffn_routes,
    ffn_logits,
    att_output_map,
    ffn_gate_up,
    ffn_down,
    norm_gain,
    out_gain,
):
    rows_dev = hidden_in.shape[0]
    model_width = hidden_in.shape[1]
    att_dim = context.shape[2]
    out_slice = att_output_map.shape[2]
    hid_slice = ffn_gate_up.shape[3]
    n_ez = lax.axis_size("ez")
    n_ey = lax.axis_size("ey")
    capacity = CAP

    att_matrix = lax.all_gather(att_output_map, "dp", axis=1, tiled=True)[0]
    gate_matrix = lax.all_gather(ffn_gate_up, "dp", axis=1, tiled=True)[0]
    down_matrix = lax.all_gather(ffn_down, "dp", axis=2, tiled=True)[0]

    att_weight = pair_weights(att_logits, att_routes)
    att_place = slot_matrix(att_routes, capacity, EXPERTS)
    outgoing = jnp.dot(
        att_place.astype(jnp.bfloat16),
        context.reshape(-1, att_dim),
        preferred_element_type=jnp.float32,
    ).astype(jnp.bfloat16)
    incoming = dispatch(outgoing.reshape(capacity, EXPERTS, att_dim))
    mapped = jnp.dot(
        incoming.reshape(-1, att_dim), att_matrix, preferred_element_type=jnp.float32
    ).astype(jnp.bfloat16)
    mapped = mapped.reshape(CORES, n_ey, capacity, n_ez, out_slice)
    me = lax.axis_index("ey")
    twice = jnp.concatenate([mapped, mapped], axis=1)
    mapped = lax.dynamic_slice_in_dim(twice, (n_ey - me) % n_ey, n_ey, axis=1)
    mapped = jnp.transpose(mapped, (3, 1, 0, 2, 4)).reshape(
        n_ez * n_ey * CORES, capacity, out_slice
    )
    back = lax.all_to_all(mapped, ("ez", "ey", "ec"), split_axis=0, concat_axis=0, tiled=True)
    back = back.reshape(EXPERTS, n_ey * CORES, capacity, out_slice)
    back = jnp.transpose(back, (2, 0, 1, 3)).reshape(capacity * EXPERTS, model_width)
    picked = jnp.dot(
        att_place.T.astype(jnp.bfloat16), back, preferred_element_type=jnp.float32
    )
    picked = picked.reshape(rows_dev, 2, model_width)
    hidden_state = (
        hidden_in.astype(jnp.float32)
        + att_weight[:, 0:1] * picked[:, 0]
        + att_weight[:, 1:2] * picked[:, 1]
    )
    ffn_in = norm_rows(hidden_state, norm_gain).astype(jnp.bfloat16)
    ffn_place = slot_matrix(ffn_routes, capacity, EXPERTS)
    row_place = jnp.any(ffn_place.reshape(EXPERTS * capacity, rows_dev, 2), axis=2)
    outgoing_rows = jnp.dot(
        row_place.astype(jnp.bfloat16), ffn_in, preferred_element_type=jnp.float32
    ).astype(jnp.bfloat16)
    incoming = dispatch(outgoing_rows.reshape(capacity, EXPERTS, model_width))
    flattened = incoming.reshape(-1, model_width)
    depth = gate_matrix.shape[0]
    gate_up = jnp.dot(
        flattened, gate_matrix.reshape(depth, 2 * hid_slice), preferred_element_type=jnp.float32
    )
    gate_up = gate_up.reshape(-1, 2, hid_slice)
    activated = (jax.nn.silu(gate_up[:, 0]) * gate_up[:, 1]).astype(jnp.bfloat16)
    projected = jnp.dot(
        activated, down_matrix, preferred_element_type=jnp.float32
    ).astype(jnp.bfloat16)
    projected = projected.reshape(CORES, n_ey * capacity * n_ez, model_width)
    reduced = lax.psum_scatter(projected, "ec", scatter_dimension=0, tiled=True)[0]
    reduced = reduced.reshape(n_ey, capacity * n_ez, model_width).astype(jnp.float32)
    reduced = ring_sums(reduced).astype(jnp.bfloat16)
    reduced = reduced.reshape(capacity, n_ez, model_width)
    summed = lax.all_to_all(reduced, "ez", split_axis=1, concat_axis=1, tiled=True)
    summed = summed.reshape(capacity * EXPERTS, model_width).astype(jnp.float32)
    ffn_weight = pair_weights(ffn_logits, ffn_routes)
    weighted = ffn_place.astype(jnp.float32) * ffn_weight.reshape(1, -1)
    expert_mix = jnp.dot(weighted.T, summed, precision=lax.Precision.HIGHEST).reshape(
        rows_dev, 2, model_width
    )
    mixed_sum = hidden_state + (expert_mix[:, 0] + expert_mix[:, 1])
    return norm_rows(mixed_sum, out_gain).astype(jnp.bfloat16)


def solution(mesh):
    n_dp = mesh.devices.shape[0]
    n_expert = mesh.devices.shape[1]
    n_ey = n_expert // (EXPERTS * CORES)
    grid = Mesh(
        mesh.devices.reshape(n_dp, EXPERTS, n_ey, CORES), ("dp", "ez", "ey", "ec")
    )
    rows = ("dp", "ez", "ey", "ec")
    owners = ("ez", "ey", "ec")
    return jax.shard_map(
        local,
        mesh=grid,
        in_specs=(
            P(rows, None),
            P(rows, None, None),
            P(rows, None),
            P(rows, None),
            P(rows, None),
            P(rows, None),
            P(owners, "dp", None),
            P(owners, "dp", None, None),
            P(owners, None, "dp"),
            P(),
            P(),
        ),
        out_specs=P(rows, None),
        check_vma=False,
    )
```

```python
import jax
import jax.numpy as jnp
from jax import lax
from jax.sharding import Mesh
from jax.sharding import PartitionSpec as P

EXPERTS = 8
CAP = 20
CORES = 2


EPSILON = 1e-06


def norm_rows(values, gain):
    mean_square = jnp.mean(values * values, axis=-1, keepdims=True)
    return values * lax.rsqrt(mean_square + EPSILON) * gain.astype(jnp.float32)


def pair_weights(logits, routes):
    expert_ids = jnp.arange(logits.shape[1], dtype=jnp.int32)
    selected = routes[:, :, None] == expert_ids[None, None, :]
    chosen = jnp.sum(jnp.where(selected, logits[:, None, :], 0.0), axis=2)
    first_weight = jax.nn.sigmoid(chosen[:, 0] - chosen[:, 1])
    return jnp.stack([first_weight, 1.0 - first_weight], axis=1)


def slot_matrix(routes, capacity, experts):
    route_list = routes.reshape(-1)
    onehot = (route_list[:, None] == jnp.arange(experts, dtype=jnp.int32)[None, :]).astype(
        jnp.int32
    )
    before = jnp.cumsum(onehot, axis=0) - onehot
    slot_index = jnp.sum(before * onehot, axis=1)
    target = slot_index * experts + route_list
    slot_ids = jnp.arange(experts * capacity, dtype=jnp.int32)
    return slot_ids[:, None] == target[None, :]


def from_left(x):
    n = lax.axis_size("ey")
    return lax.ppermute(x, "ey", [(i, (i + 1) % n) for i in range(n)])


def from_right(x):
    n = lax.axis_size("ey")
    return lax.ppermute(x, "ey", [(i, (i - 1) % n) for i in range(n)])


def ring_copies(block):
    half = block.shape[0] // 2
    left = from_left(block)
    right = from_right(block)
    far = jnp.concatenate([from_left(left[:half]), from_right(right[half:])], axis=0)
    return jnp.stack([block, right, far, left], axis=0)


def ring_sums(parts):
    half = parts.shape[1] // 2
    far = parts[2].astype(jnp.bfloat16)
    early_right = from_right(far[:half]).astype(jnp.float32)
    early_left = from_left(far[half:]).astype(jnp.float32)
    to_left = jnp.concatenate([parts[3, :half] + early_right, parts[3, half:]], axis=0)
    to_right = jnp.concatenate([parts[1, :half], parts[1, half:] + early_left], axis=0)
    got_right = from_right(to_left.astype(jnp.bfloat16)).astype(jnp.float32)
    got_left = from_left(to_right.astype(jnp.bfloat16)).astype(jnp.float32)
    return parts[0] + got_right + got_left


def dispatch(blocks):
    arrived = lax.all_to_all(blocks, "ez", split_axis=1, concat_axis=1, tiled=True)
    return ring_copies(arrived)


def chip_pair(weights):
    core = lax.axis_index("ec")
    other = lax.ppermute(weights, "ec", [(0, 1), (1, 0)])
    first = jnp.where(core == 0, weights, other)
    second = jnp.where(core == 0, other, weights)
    return first, second


def local(
    hidden_in,
    context,
    att_routes,
    att_logits,
    ffn_routes,
    ffn_logits,
    att_output_map,
    ffn_gate_up,
    ffn_down,
    norm_gain,
    out_gain,
):
    rows_dev = hidden_in.shape[0]
    model_width = hidden_in.shape[1]
    att_dim = context.shape[2]
    out_slice = att_output_map.shape[2]
    hid_slice = ffn_gate_up.shape[3]
    n_ez = lax.axis_size("ez")
    n_ey = lax.axis_size("ey")
    capacity = CAP

    att_matrix = lax.all_gather(att_output_map, "dp", axis=1, tiled=True)[0]
    gate_matrix = lax.all_gather(ffn_gate_up, "dp", axis=1, tiled=True)[0]
    down_matrix = lax.all_gather(ffn_down, "dp", axis=2, tiled=True)[0]
    att_first, att_second = chip_pair(att_matrix)

    att_weight = pair_weights(att_logits, att_routes)
    att_place = slot_matrix(att_routes, capacity, EXPERTS)
    outgoing = jnp.dot(
        att_place.astype(jnp.bfloat16),
        context.reshape(-1, att_dim),
        preferred_element_type=jnp.float32,
    ).astype(jnp.bfloat16)
    incoming = dispatch(outgoing.reshape(capacity, EXPERTS, att_dim))
    mapped = jnp.dot(
        incoming.reshape(-1, att_dim),
        jnp.concatenate([att_first, att_second], axis=1),
        preferred_element_type=jnp.float32,
    ).astype(jnp.bfloat16)
    pair_width = CORES * out_slice
    mapped = mapped.reshape(n_ey, capacity, n_ez, pair_width)
    me = lax.axis_index("ey")
    twice = jnp.concatenate([mapped, mapped], axis=0)
    mapped = lax.dynamic_slice_in_dim(twice, (n_ey - me) % n_ey, n_ey, axis=0)
    mapped = jnp.transpose(mapped, (2, 0, 1, 3)).reshape(n_ez * n_ey, capacity, pair_width)
    back = lax.all_to_all(mapped, ("ez", "ey"), split_axis=0, concat_axis=0, tiled=True)
    back = back.reshape(EXPERTS, n_ey, capacity, pair_width)
    back = jnp.transpose(back, (2, 0, 1, 3)).reshape(capacity * EXPERTS, model_width)
    picked = jnp.dot(
        att_place.T.astype(jnp.bfloat16), back, preferred_element_type=jnp.float32
    )
    gate_matrix, _ = lax.optimization_barrier((gate_matrix, picked))
    depth = gate_matrix.shape[0]
    gate_first, gate_second = chip_pair(gate_matrix.reshape(depth, 2 * hid_slice))
    picked = picked.reshape(rows_dev, 2, model_width)
    hidden_state = (
        hidden_in.astype(jnp.float32)
        + att_weight[:, 0:1] * picked[:, 0]
        + att_weight[:, 1:2] * picked[:, 1]
    )
    ffn_in = norm_rows(hidden_state, norm_gain).astype(jnp.bfloat16)
    ffn_place = slot_matrix(ffn_routes, capacity, EXPERTS)
    row_place = jnp.any(ffn_place.reshape(EXPERTS * capacity, rows_dev, 2), axis=2)
    outgoing_rows = jnp.dot(
        row_place.astype(jnp.bfloat16), ffn_in, preferred_element_type=jnp.float32
    ).astype(jnp.bfloat16)
    incoming = dispatch(outgoing_rows.reshape(capacity, EXPERTS, model_width))
    flattened = incoming.reshape(-1, model_width)
    down_matrix, _ = lax.optimization_barrier((down_matrix, incoming))
    down_first, down_second = chip_pair(down_matrix)
    gate_up = jnp.dot(
        flattened,
        jnp.concatenate([gate_first, gate_second], axis=1),
        preferred_element_type=jnp.float32,
    )
    gate_up = gate_up.reshape(-1, CORES, 2, hid_slice)
    activated = (jax.nn.silu(gate_up[:, :, 0]) * gate_up[:, :, 1]).astype(jnp.bfloat16)
    projected = jnp.einsum(
        "rjk,jkd->jrd",
        activated,
        jnp.stack([down_first, down_second], axis=0),
        preferred_element_type=jnp.float32,
    ).astype(jnp.bfloat16)
    projected = jnp.sum(projected.astype(jnp.float32), axis=0)
    reduced = projected.reshape(n_ey, capacity * n_ez, model_width)
    reduced = ring_sums(reduced).astype(jnp.bfloat16)
    reduced = reduced.reshape(capacity, n_ez, model_width)
    summed = lax.all_to_all(reduced, "ez", split_axis=1, concat_axis=1, tiled=True)
    summed = summed.reshape(capacity * EXPERTS, model_width).astype(jnp.float32)
    ffn_weight = pair_weights(ffn_logits, ffn_routes)
    weighted = ffn_place.astype(jnp.float32) * ffn_weight.reshape(1, -1)
    expert_mix = jnp.dot(weighted.T, summed, precision=lax.Precision.HIGHEST).reshape(
        rows_dev, 2, model_width
    )
    mixed_sum = hidden_state + (expert_mix[:, 0] + expert_mix[:, 1])
    return norm_rows(mixed_sum, out_gain).astype(jnp.bfloat16)


def solution(mesh):
    n_dp = mesh.devices.shape[0]
    n_expert = mesh.devices.shape[1]
    n_ey = n_expert // (EXPERTS * CORES)
    grid = Mesh(
        mesh.devices.reshape(n_dp, EXPERTS, n_ey, CORES), ("dp", "ez", "ey", "ec")
    )
    rows = ("dp", "ez", "ey", "ec")
    owners = ("ez", "ey", "ec")
    return jax.shard_map(
        local,
        mesh=grid,
        in_specs=(
            P(rows, None),
            P(rows, None, None),
            P(rows, None),
            P(rows, None),
            P(rows, None),
            P(rows, None),
            P(owners, "dp", None),
            P(owners, "dp", None, None),
            P(owners, None, "dp"),
            P(),
            P(),
        ),
        out_specs=P(rows, None),
        check_vma=False,
    )
```

```python
import jax
import jax.numpy as jnp
from jax import lax
from jax.sharding import Mesh
from jax.sharding import PartitionSpec as P

EXPERTS = 8
CAP = 20
CORES = 2


EPSILON = 1e-06


def norm_rows(values, gain):
    mean_square = jnp.mean(values * values, axis=-1, keepdims=True)
    return values * lax.rsqrt(mean_square + EPSILON) * gain.astype(jnp.float32)


def pair_weights(logits, routes):
    expert_ids = jnp.arange(logits.shape[1], dtype=jnp.int32)
    selected = routes[:, :, None] == expert_ids[None, None, :]
    chosen = jnp.sum(jnp.where(selected, logits[:, None, :], 0.0), axis=2)
    first_weight = jax.nn.sigmoid(chosen[:, 0] - chosen[:, 1])
    return jnp.stack([first_weight, 1.0 - first_weight], axis=1)


def slot_matrix(routes, capacity, experts):
    route_list = routes.reshape(-1)
    onehot = (route_list[:, None] == jnp.arange(experts, dtype=jnp.int32)[None, :]).astype(
        jnp.int32
    )
    before = jnp.cumsum(onehot, axis=0) - onehot
    slot_index = jnp.sum(before * onehot, axis=1)
    target = slot_index * experts + route_list
    slot_ids = jnp.arange(experts * capacity, dtype=jnp.int32)
    return slot_ids[:, None] == target[None, :]


def from_left(x):
    n = lax.axis_size("ey")
    return lax.ppermute(x, "ey", [(i, (i + 1) % n) for i in range(n)])


def from_right(x):
    n = lax.axis_size("ey")
    return lax.ppermute(x, "ey", [(i, (i - 1) % n) for i in range(n)])


def ring_copies(block):
    half = block.shape[0] // 2
    left = from_left(block)
    right = from_right(block)
    far = jnp.concatenate([from_left(left[:half]), from_right(right[half:])], axis=0)
    return jnp.stack([block, right, far, left], axis=0)


def ring_sums(parts):
    half = parts.shape[1] // 2
    far = parts[2].astype(jnp.bfloat16)
    early_right = from_right(far[:half]).astype(jnp.float32)
    early_left = from_left(far[half:]).astype(jnp.float32)
    to_left = jnp.concatenate([parts[3, :half] + early_right, parts[3, half:]], axis=0)
    to_right = jnp.concatenate([parts[1, :half], parts[1, half:] + early_left], axis=0)
    got_right = from_right(to_left.astype(jnp.bfloat16)).astype(jnp.float32)
    got_left = from_left(to_right.astype(jnp.bfloat16)).astype(jnp.float32)
    return parts[0] + got_right + got_left


def dispatch(blocks):
    arrived = lax.all_to_all(blocks, "ez", split_axis=1, concat_axis=1, tiled=True)
    return ring_copies(arrived)


def chip_pair(weights):
    return weights, lax.ppermute(weights, "ec", [(0, 1), (1, 0)])


def local(
    hidden_in,
    context,
    att_routes,
    att_logits,
    ffn_routes,
    ffn_logits,
    att_output_map,
    ffn_gate_up,
    ffn_down,
    norm_gain,
    out_gain,
):
    rows_dev = hidden_in.shape[0]
    model_width = hidden_in.shape[1]
    att_dim = context.shape[2]
    out_slice = att_output_map.shape[2]
    hid_slice = ffn_gate_up.shape[3]
    n_ez = lax.axis_size("ez")
    n_ey = lax.axis_size("ey")
    capacity = CAP

    att_matrix = lax.all_gather(att_output_map, "dp", axis=1, tiled=True)[0]
    gate_matrix = lax.all_gather(ffn_gate_up, "dp", axis=1, tiled=True)[0]
    down_matrix = lax.all_gather(ffn_down, "dp", axis=2, tiled=True)[0]
    att_own, att_other = chip_pair(att_matrix)

    att_weight = pair_weights(att_logits, att_routes)
    att_place = slot_matrix(att_routes, capacity, EXPERTS)
    outgoing = jnp.dot(
        att_place.astype(jnp.bfloat16),
        context.reshape(-1, att_dim),
        preferred_element_type=jnp.float32,
    ).astype(jnp.bfloat16)
    incoming = dispatch(outgoing.reshape(capacity, EXPERTS, att_dim))
    rows_in = incoming.reshape(-1, att_dim)
    mapped = jnp.stack(
        [
            jnp.dot(rows_in, att_own, preferred_element_type=jnp.float32),
            jnp.dot(rows_in, att_other, preferred_element_type=jnp.float32),
        ],
        axis=1,
    ).astype(jnp.bfloat16)
    pair_width = CORES * out_slice
    mapped = mapped.reshape(n_ey, capacity, n_ez, pair_width)
    me = lax.axis_index("ey")
    twice = jnp.concatenate([mapped, mapped], axis=0)
    mapped = lax.dynamic_slice_in_dim(twice, (n_ey - me) % n_ey, n_ey, axis=0)
    mapped = jnp.transpose(mapped, (2, 0, 1, 3)).reshape(n_ez * n_ey, capacity, pair_width)
    back = lax.all_to_all(mapped, ("ez", "ey"), split_axis=0, concat_axis=0, tiled=True)
    back = back.reshape(EXPERTS, n_ey, capacity, CORES, out_slice)
    core = lax.axis_index("ec")
    back = jnp.where(core == 0, back, back[:, :, :, ::-1])
    back = jnp.transpose(back, (2, 0, 1, 3, 4)).reshape(capacity * EXPERTS, model_width)
    picked = jnp.dot(
        att_place.T.astype(jnp.bfloat16), back, preferred_element_type=jnp.float32
    )
    gate_matrix, _ = lax.optimization_barrier((gate_matrix, picked))
    depth = gate_matrix.shape[0]
    gate_own, gate_other = chip_pair(gate_matrix.reshape(depth, 2 * hid_slice))
    picked = picked.reshape(rows_dev, 2, model_width)
    hidden_state = (
        hidden_in.astype(jnp.float32)
        + att_weight[:, 0:1] * picked[:, 0]
        + att_weight[:, 1:2] * picked[:, 1]
    )
    ffn_in = norm_rows(hidden_state, norm_gain).astype(jnp.bfloat16)
    ffn_place = slot_matrix(ffn_routes, capacity, EXPERTS)
    row_place = jnp.any(ffn_place.reshape(EXPERTS * capacity, rows_dev, 2), axis=2)
    outgoing_rows = jnp.dot(
        row_place.astype(jnp.bfloat16), ffn_in, preferred_element_type=jnp.float32
    ).astype(jnp.bfloat16)
    incoming = dispatch(outgoing_rows.reshape(capacity, EXPERTS, model_width))
    flattened = incoming.reshape(-1, model_width)
    down_matrix, _ = lax.optimization_barrier((down_matrix, incoming))
    down_own, down_other = chip_pair(down_matrix)

    def slice_part(gate_w, down_w):
        gate_up = jnp.dot(flattened, gate_w, preferred_element_type=jnp.float32)
        gate_up = gate_up.reshape(-1, 2, hid_slice)
        activated = (jax.nn.silu(gate_up[:, 0]) * gate_up[:, 1]).astype(jnp.bfloat16)
        part = jnp.dot(activated, down_w, preferred_element_type=jnp.float32)
        return part.astype(jnp.bfloat16).astype(jnp.float32)

    projected = slice_part(gate_own, down_own) + slice_part(gate_other, down_other)
    reduced = projected.reshape(n_ey, capacity * n_ez, model_width)
    reduced = ring_sums(reduced).astype(jnp.bfloat16)
    reduced = reduced.reshape(capacity, n_ez, model_width)
    summed = lax.all_to_all(reduced, "ez", split_axis=1, concat_axis=1, tiled=True)
    summed = summed.reshape(capacity * EXPERTS, model_width).astype(jnp.float32)
    ffn_weight = pair_weights(ffn_logits, ffn_routes)
    weighted = ffn_place.astype(jnp.float32) * ffn_weight.reshape(1, -1)
    expert_mix = jnp.dot(weighted.T, summed, precision=lax.Precision.HIGHEST).reshape(
        rows_dev, 2, model_width
    )
    mixed_sum = hidden_state + (expert_mix[:, 0] + expert_mix[:, 1])
    return norm_rows(mixed_sum, out_gain).astype(jnp.bfloat16)


def solution(mesh):
    n_dp = mesh.devices.shape[0]
    n_expert = mesh.devices.shape[1]
    n_ey = n_expert // (EXPERTS * CORES)
    grid = Mesh(
        mesh.devices.reshape(n_dp, EXPERTS, n_ey, CORES), ("dp", "ez", "ey", "ec")
    )
    rows = ("dp", "ez", "ey", "ec")
    owners = ("ez", "ey", "ec")
    return jax.shard_map(
        local,
        mesh=grid,
        in_specs=(
            P(rows, None),
            P(rows, None, None),
            P(rows, None),
            P(rows, None),
            P(rows, None),
            P(rows, None),
            P(owners, "dp", None),
            P(owners, "dp", None, None),
            P(owners, None, "dp"),
            P(),
            P(),
        ),
        out_specs=P(rows, None),
        check_vma=False,
    )
```

```python
import jax
import jax.numpy as jnp
from jax import lax
from jax.sharding import Mesh
from jax.sharding import PartitionSpec as P

EXPERTS = 8
CAP = 20
CORES = 2


EPSILON = 1e-06


def norm_rows(values, gain):
    mean_square = jnp.mean(values * values, axis=-1, keepdims=True)
    return values * lax.rsqrt(mean_square + EPSILON) * gain.astype(jnp.float32)


def pair_weights(logits, routes):
    expert_ids = jnp.arange(logits.shape[1], dtype=jnp.int32)
    selected = routes[:, :, None] == expert_ids[None, None, :]
    chosen = jnp.sum(jnp.where(selected, logits[:, None, :], 0.0), axis=2)
    first_weight = jax.nn.sigmoid(chosen[:, 0] - chosen[:, 1])
    return jnp.stack([first_weight, 1.0 - first_weight], axis=1)


def slot_matrix(routes, capacity, experts):
    route_list = routes.reshape(-1)
    onehot = (route_list[:, None] == jnp.arange(experts, dtype=jnp.int32)[None, :]).astype(
        jnp.int32
    )
    before = jnp.cumsum(onehot, axis=0) - onehot
    slot_index = jnp.sum(before * onehot, axis=1)
    target = slot_index * experts + route_list
    slot_ids = jnp.arange(experts * capacity, dtype=jnp.int32)
    return slot_ids[:, None] == target[None, :]


def from_left(x):
    n = lax.axis_size("ey")
    return lax.ppermute(x, "ey", [(i, (i + 1) % n) for i in range(n)])


def from_right(x):
    n = lax.axis_size("ey")
    return lax.ppermute(x, "ey", [(i, (i - 1) % n) for i in range(n)])


def ring_copies(block):
    half = block.shape[0] // 2
    left = from_left(block)
    right = from_right(block)
    far = jnp.concatenate([from_left(left[:half]), from_right(right[half:])], axis=0)
    return jnp.stack([block, right, far, left], axis=0)


def ring_sums(parts):
    half = parts.shape[1] // 2
    far = parts[2].astype(jnp.bfloat16)
    early_right = from_right(far[:half]).astype(jnp.float32)
    early_left = from_left(far[half:]).astype(jnp.float32)
    to_left = jnp.concatenate([parts[3, :half] + early_right, parts[3, half:]], axis=0)
    to_right = jnp.concatenate([parts[1, :half], parts[1, half:] + early_left], axis=0)
    got_right = from_right(to_left.astype(jnp.bfloat16)).astype(jnp.float32)
    got_left = from_left(to_right.astype(jnp.bfloat16)).astype(jnp.float32)
    return parts[0] + got_right + got_left


def dispatch(blocks):
    arrived = lax.all_to_all(blocks, "ez", split_axis=1, concat_axis=1, tiled=True)
    return ring_copies(arrived)


def chip_pair(weights):
    return weights, lax.ppermute(weights, "ec", [(0, 1), (1, 0)])


def local(
    hidden_in,
    context,
    att_routes,
    att_logits,
    ffn_routes,
    ffn_logits,
    att_output_map,
    ffn_gate_up,
    ffn_down,
    norm_gain,
    out_gain,
):
    rows_dev = hidden_in.shape[0]
    model_width = hidden_in.shape[1]
    att_dim = context.shape[2]
    out_slice = att_output_map.shape[2]
    hid_slice = ffn_gate_up.shape[3]
    n_ez = lax.axis_size("ez")
    n_ey = lax.axis_size("ey")
    capacity = CAP

    att_matrix = lax.all_gather(att_output_map, "dp", axis=1, tiled=True)[0]
    gate_matrix = lax.all_gather(ffn_gate_up, "dp", axis=1, tiled=True)[0]
    down_matrix = lax.all_gather(ffn_down, "dp", axis=2, tiled=True)[0]
    att_own, att_other = chip_pair(att_matrix)
    core = lax.axis_index("ec")
    att_first = jnp.where(core == 0, att_own, att_other)
    att_second = jnp.where(core == 0, att_other, att_own)

    att_weight = pair_weights(att_logits, att_routes)
    att_place = slot_matrix(att_routes, capacity, EXPERTS)
    outgoing = jnp.dot(
        att_place.astype(jnp.bfloat16),
        context.reshape(-1, att_dim),
        preferred_element_type=jnp.float32,
    ).astype(jnp.bfloat16)
    incoming = dispatch(outgoing.reshape(capacity, EXPERTS, att_dim))
    rows_in = incoming.reshape(-1, att_dim)
    mapped = jnp.stack(
        [
            jnp.dot(rows_in, att_first, preferred_element_type=jnp.float32),
            jnp.dot(rows_in, att_second, preferred_element_type=jnp.float32),
        ],
        axis=1,
    ).astype(jnp.bfloat16)
    pair_width = CORES * out_slice
    mapped = mapped.reshape(n_ey, capacity, n_ez, pair_width)
    me = lax.axis_index("ey")
    twice = jnp.concatenate([mapped, mapped], axis=0)
    mapped = lax.dynamic_slice_in_dim(twice, (n_ey - me) % n_ey, n_ey, axis=0)
    mapped = jnp.transpose(mapped, (2, 0, 1, 3)).reshape(n_ez * n_ey, capacity, pair_width)
    back = lax.all_to_all(mapped, ("ez", "ey"), split_axis=0, concat_axis=0, tiled=True)
    back = back.reshape(EXPERTS, n_ey, capacity, pair_width)
    back = jnp.transpose(back, (2, 0, 1, 3)).reshape(capacity * EXPERTS, model_width)
    picked = jnp.dot(
        att_place.T.astype(jnp.bfloat16), back, preferred_element_type=jnp.float32
    )
    gate_matrix, _ = lax.optimization_barrier((gate_matrix, picked))
    depth = gate_matrix.shape[0]
    gate_own, gate_other = chip_pair(gate_matrix.reshape(depth, 2 * hid_slice))
    picked = picked.reshape(rows_dev, 2, model_width)
    hidden_state = (
        hidden_in.astype(jnp.float32)
        + att_weight[:, 0:1] * picked[:, 0]
        + att_weight[:, 1:2] * picked[:, 1]
    )
    ffn_in = norm_rows(hidden_state, norm_gain).astype(jnp.bfloat16)
    ffn_place = slot_matrix(ffn_routes, capacity, EXPERTS)
    row_place = jnp.any(ffn_place.reshape(EXPERTS * capacity, rows_dev, 2), axis=2)
    outgoing_rows = jnp.dot(
        row_place.astype(jnp.bfloat16), ffn_in, preferred_element_type=jnp.float32
    ).astype(jnp.bfloat16)
    incoming = dispatch(outgoing_rows.reshape(capacity, EXPERTS, model_width))
    flattened = incoming.reshape(-1, model_width)
    down_matrix, _ = lax.optimization_barrier((down_matrix, incoming))
    down_own, down_other = chip_pair(down_matrix)

    def slice_part(gate_w, down_w):
        gate_up = jnp.dot(flattened, gate_w, preferred_element_type=jnp.float32)
        gate_up = gate_up.reshape(-1, 2, hid_slice)
        activated = (jax.nn.silu(gate_up[:, 0]) * gate_up[:, 1]).astype(jnp.bfloat16)
        part = jnp.dot(activated, down_w, preferred_element_type=jnp.float32)
        return part.astype(jnp.bfloat16).astype(jnp.float32)

    projected = slice_part(gate_own, down_own) + slice_part(gate_other, down_other)
    reduced = projected.reshape(n_ey, capacity * n_ez, model_width)
    reduced = ring_sums(reduced).astype(jnp.bfloat16)
    reduced = reduced.reshape(capacity, n_ez, model_width)
    summed = lax.all_to_all(reduced, "ez", split_axis=1, concat_axis=1, tiled=True)
    summed = summed.reshape(capacity * EXPERTS, model_width).astype(jnp.float32)
    ffn_weight = pair_weights(ffn_logits, ffn_routes)
    weighted = ffn_place.astype(jnp.float32) * ffn_weight.reshape(1, -1)
    expert_mix = jnp.dot(weighted.T, summed, precision=lax.Precision.HIGHEST).reshape(
        rows_dev, 2, model_width
    )
    mixed_sum = hidden_state + (expert_mix[:, 0] + expert_mix[:, 1])
    return norm_rows(mixed_sum, out_gain).astype(jnp.bfloat16)


def solution(mesh):
    n_dp = mesh.devices.shape[0]
    n_expert = mesh.devices.shape[1]
    n_ey = n_expert // (EXPERTS * CORES)
    grid = Mesh(
        mesh.devices.reshape(n_dp, EXPERTS, n_ey, CORES), ("dp", "ez", "ey", "ec")
    )
    rows = ("dp", "ez", "ey", "ec")
    owners = ("ez", "ey", "ec")
    return jax.shard_map(
        local,
        mesh=grid,
        in_specs=(
            P(rows, None),
            P(rows, None, None),
            P(rows, None),
            P(rows, None),
            P(rows, None),
            P(rows, None),
            P(owners, "dp", None),
            P(owners, "dp", None, None),
            P(owners, None, "dp"),
            P(),
            P(),
        ),
        out_specs=P(rows, None),
        check_vma=False,
    )
```

```python
import jax
import jax.numpy as jnp
from jax import lax
from jax.sharding import Mesh
from jax.sharding import PartitionSpec as P

EXPERTS = 8
CAP = 20
CORES = 2


EPSILON = 1e-06


def norm_rows(values, gain):
    mean_square = jnp.mean(values * values, axis=-1, keepdims=True)
    return values * lax.rsqrt(mean_square + EPSILON) * gain.astype(jnp.float32)


def pair_weights(logits, routes):
    expert_ids = jnp.arange(logits.shape[1], dtype=jnp.int32)
    selected = routes[:, :, None] == expert_ids[None, None, :]
    chosen = jnp.sum(jnp.where(selected, logits[:, None, :], 0.0), axis=2)
    first_weight = jax.nn.sigmoid(chosen[:, 0] - chosen[:, 1])
    return jnp.stack([first_weight, 1.0 - first_weight], axis=1)


def slot_matrix(routes, capacity, experts):
    route_list = routes.reshape(-1)
    onehot = (route_list[:, None] == jnp.arange(experts, dtype=jnp.int32)[None, :]).astype(
        jnp.int32
    )
    before = jnp.cumsum(onehot, axis=0) - onehot
    slot_index = jnp.sum(before * onehot, axis=1)
    target = slot_index * experts + route_list
    slot_ids = jnp.arange(experts * capacity, dtype=jnp.int32)
    return slot_ids[:, None] == target[None, :]


def from_left(x):
    n = lax.axis_size("ey")
    return lax.ppermute(x, "ey", [(i, (i + 1) % n) for i in range(n)])


def from_right(x):
    n = lax.axis_size("ey")
    return lax.ppermute(x, "ey", [(i, (i - 1) % n) for i in range(n)])


def ring_blocks(block):
    half = block.shape[0] // 2
    left = from_left(block)
    right = from_right(block)
    far = jnp.concatenate([from_left(left[:half]), from_right(right[half:])], axis=0)
    return block, right, far, left


def ring_copies(block):
    return jnp.stack(ring_blocks(block), axis=0)


def ring_sums(parts):
    half = parts[2].shape[0] // 2
    far = parts[2].astype(jnp.bfloat16)
    early_right = from_right(far[:half]).astype(jnp.float32)
    early_left = from_left(far[half:]).astype(jnp.float32)
    to_left = jnp.concatenate([parts[3][:half] + early_right, parts[3][half:]], axis=0)
    to_right = jnp.concatenate([parts[1][:half], parts[1][half:] + early_left], axis=0)
    got_right = from_right(to_left.astype(jnp.bfloat16)).astype(jnp.float32)
    got_left = from_left(to_right.astype(jnp.bfloat16)).astype(jnp.float32)
    return parts[0] + got_right + got_left


def dispatch(blocks):
    arrived = lax.all_to_all(blocks, "ez", split_axis=1, concat_axis=1, tiled=True)
    return ring_copies(arrived)


def chip_pair(weights):
    return weights, lax.ppermute(weights, "ec", [(0, 1), (1, 0)])


def local(
    hidden_in,
    context,
    att_routes,
    att_logits,
    ffn_routes,
    ffn_logits,
    att_output_map,
    ffn_gate_up,
    ffn_down,
    norm_gain,
    out_gain,
):
    rows_dev = hidden_in.shape[0]
    model_width = hidden_in.shape[1]
    att_dim = context.shape[2]
    out_slice = att_output_map.shape[2]
    hid_slice = ffn_gate_up.shape[3]
    n_ez = lax.axis_size("ez")
    n_ey = lax.axis_size("ey")
    capacity = CAP

    att_matrix = lax.all_gather(att_output_map, "dp", axis=1, tiled=True)[0]
    gate_matrix = lax.all_gather(ffn_gate_up, "dp", axis=1, tiled=True)[0]
    down_matrix = lax.all_gather(ffn_down, "dp", axis=2, tiled=True)[0]
    att_own, att_other = chip_pair(att_matrix)
    core = lax.axis_index("ec")
    att_first = jnp.where(core == 0, att_own, att_other)
    att_second = jnp.where(core == 0, att_other, att_own)

    att_weight = pair_weights(att_logits, att_routes)
    att_place = slot_matrix(att_routes, capacity, EXPERTS)
    outgoing = jnp.dot(
        att_place.astype(jnp.bfloat16),
        context.reshape(-1, att_dim),
        preferred_element_type=jnp.float32,
    ).astype(jnp.bfloat16)
    incoming = dispatch(outgoing.reshape(capacity, EXPERTS, att_dim))
    rows_in = incoming.reshape(-1, att_dim)
    mapped = jnp.stack(
        [
            jnp.dot(rows_in, att_first, preferred_element_type=jnp.float32),
            jnp.dot(rows_in, att_second, preferred_element_type=jnp.float32),
        ],
        axis=1,
    ).astype(jnp.bfloat16)
    pair_width = CORES * out_slice
    mapped = mapped.reshape(n_ey, capacity, n_ez, pair_width)
    me = lax.axis_index("ey")
    twice = jnp.concatenate([mapped, mapped], axis=0)
    mapped = lax.dynamic_slice_in_dim(twice, (n_ey - me) % n_ey, n_ey, axis=0)
    mapped = jnp.transpose(mapped, (2, 0, 1, 3)).reshape(n_ez * n_ey, capacity, pair_width)
    back = lax.all_to_all(mapped, ("ez", "ey"), split_axis=0, concat_axis=0, tiled=True)
    back = back.reshape(EXPERTS, n_ey, capacity, pair_width)
    back = jnp.transpose(back, (2, 0, 1, 3)).reshape(capacity * EXPERTS, model_width)
    picked = jnp.dot(
        att_place.T.astype(jnp.bfloat16), back, preferred_element_type=jnp.float32
    )
    gate_matrix, _ = lax.optimization_barrier((gate_matrix, picked))
    depth = gate_matrix.shape[0]
    gate_own, gate_other = chip_pair(gate_matrix.reshape(depth, 2 * hid_slice))
    picked = picked.reshape(rows_dev, 2, model_width)
    hidden_state = (
        hidden_in.astype(jnp.float32)
        + att_weight[:, 0:1] * picked[:, 0]
        + att_weight[:, 1:2] * picked[:, 1]
    )
    ffn_in = norm_rows(hidden_state, norm_gain).astype(jnp.bfloat16)
    ffn_place = slot_matrix(ffn_routes, capacity, EXPERTS)
    row_place = jnp.any(ffn_place.reshape(EXPERTS * capacity, rows_dev, 2), axis=2)
    outgoing_rows = jnp.dot(
        row_place.astype(jnp.bfloat16), ffn_in, preferred_element_type=jnp.float32
    ).astype(jnp.bfloat16)
    arrived = lax.all_to_all(
        outgoing_rows.reshape(capacity, EXPERTS, model_width),
        "ez",
        split_axis=1,
        concat_axis=1,
        tiled=True,
    )
    blocks = [b.reshape(-1, model_width) for b in ring_blocks(arrived)]
    down_matrix, _ = lax.optimization_barrier((down_matrix, blocks[2]))
    down_own, down_other = chip_pair(down_matrix)

    def slice_part(rows, gate_w, down_w):
        gate_up = jnp.dot(rows, gate_w, preferred_element_type=jnp.float32)
        gate_up = gate_up.reshape(-1, 2, hid_slice)
        activated = (jax.nn.silu(gate_up[:, 0]) * gate_up[:, 1]).astype(jnp.bfloat16)
        part = jnp.dot(activated, down_w, preferred_element_type=jnp.float32)
        return part.astype(jnp.bfloat16).astype(jnp.float32)

    own_terms = [slice_part(b, gate_own, down_own) for b in blocks]
    parts = [own_terms[r] + slice_part(blocks[r], gate_other, down_other) for r in range(4)]
    reduced = ring_sums(parts).astype(jnp.bfloat16)
    reduced = reduced.reshape(capacity, n_ez, model_width)
    summed = lax.all_to_all(reduced, "ez", split_axis=1, concat_axis=1, tiled=True)
    summed = summed.reshape(capacity * EXPERTS, model_width).astype(jnp.float32)
    ffn_weight = pair_weights(ffn_logits, ffn_routes)
    weighted = ffn_place.astype(jnp.float32) * ffn_weight.reshape(1, -1)
    expert_mix = jnp.dot(weighted.T, summed, precision=lax.Precision.HIGHEST).reshape(
        rows_dev, 2, model_width
    )
    mixed_sum = hidden_state + (expert_mix[:, 0] + expert_mix[:, 1])
    return norm_rows(mixed_sum, out_gain).astype(jnp.bfloat16)


def solution(mesh):
    n_dp = mesh.devices.shape[0]
    n_expert = mesh.devices.shape[1]
    n_ey = n_expert // (EXPERTS * CORES)
    grid = Mesh(
        mesh.devices.reshape(n_dp, EXPERTS, n_ey, CORES), ("dp", "ez", "ey", "ec")
    )
    rows = ("dp", "ez", "ey", "ec")
    owners = ("ez", "ey", "ec")
    return jax.shard_map(
        local,
        mesh=grid,
        in_specs=(
            P(rows, None),
            P(rows, None, None),
            P(rows, None),
            P(rows, None),
            P(rows, None),
            P(rows, None),
            P(owners, "dp", None),
            P(owners, "dp", None, None),
            P(owners, None, "dp"),
            P(),
            P(),
        ),
        out_specs=P(rows, None),
        check_vma=False,
    )
```

```python
import jax
import jax.numpy as jnp
from jax import lax
from jax.sharding import Mesh
from jax.sharding import PartitionSpec as P

EXPERTS = 8
CAP = 20
CORES = 2


EPSILON = 1e-06


def norm_rows(values, gain):
    mean_square = jnp.mean(values * values, axis=-1, keepdims=True)
    return values * lax.rsqrt(mean_square + EPSILON) * gain.astype(jnp.float32)


def pair_weights(logits, routes):
    expert_ids = jnp.arange(logits.shape[1], dtype=jnp.int32)
    selected = routes[:, :, None] == expert_ids[None, None, :]
    chosen = jnp.sum(jnp.where(selected, logits[:, None, :], 0.0), axis=2)
    first_weight = jax.nn.sigmoid(chosen[:, 0] - chosen[:, 1])
    return jnp.stack([first_weight, 1.0 - first_weight], axis=1)


def slot_matrix(routes, capacity, experts):
    route_list = routes.reshape(-1)
    onehot = (route_list[:, None] == jnp.arange(experts, dtype=jnp.int32)[None, :]).astype(
        jnp.int32
    )
    before = jnp.cumsum(onehot, axis=0) - onehot
    slot_index = jnp.sum(before * onehot, axis=1)
    target = slot_index * experts + route_list
    slot_ids = jnp.arange(experts * capacity, dtype=jnp.int32)
    return slot_ids[:, None] == target[None, :]


def from_left(x):
    n = lax.axis_size("ey")
    return lax.ppermute(x, "ey", [(i, (i + 1) % n) for i in range(n)])


def from_right(x):
    n = lax.axis_size("ey")
    return lax.ppermute(x, "ey", [(i, (i - 1) % n) for i in range(n)])


def ring_blocks(block):
    half = block.shape[0] // 2
    left = from_left(block)
    right = from_right(block)
    far = jnp.concatenate([from_left(left[:half]), from_right(right[half:])], axis=0)
    return block, right, far, left


def ring_copies(block):
    return jnp.stack(ring_blocks(block), axis=0)


def ring_sums(parts):
    half = parts[2].shape[0] // 2
    far = parts[2].astype(jnp.bfloat16)
    early_right = from_right(far[:half]).astype(jnp.float32)
    early_left = from_left(far[half:]).astype(jnp.float32)
    to_left = jnp.concatenate([parts[3][:half] + early_right, parts[3][half:]], axis=0)
    to_right = jnp.concatenate([parts[1][:half], parts[1][half:] + early_left], axis=0)
    got_right = from_right(to_left.astype(jnp.bfloat16)).astype(jnp.float32)
    got_left = from_left(to_right.astype(jnp.bfloat16)).astype(jnp.float32)
    return parts[0] + got_right + got_left


def dispatch(blocks):
    arrived = lax.all_to_all(blocks, "ez", split_axis=1, concat_axis=1, tiled=True)
    return ring_copies(arrived)


def chip_pair(weights):
    return weights, lax.ppermute(weights, "ec", [(0, 1), (1, 0)])


def local(
    hidden_in,
    context,
    att_routes,
    att_logits,
    ffn_routes,
    ffn_logits,
    att_output_map,
    ffn_gate_up,
    ffn_down,
    norm_gain,
    out_gain,
):
    rows_dev = hidden_in.shape[0]
    model_width = hidden_in.shape[1]
    att_dim = context.shape[2]
    out_slice = att_output_map.shape[2]
    hid_slice = ffn_gate_up.shape[3]
    n_ez = lax.axis_size("ez")
    n_ey = lax.axis_size("ey")
    capacity = CAP

    att_matrix = lax.all_gather(att_output_map, "dp", axis=1, tiled=True)[0]
    gate_matrix = lax.all_gather(ffn_gate_up, "dp", axis=1, tiled=True)[0]
    down_matrix = lax.all_gather(ffn_down, "dp", axis=2, tiled=True)[0]
    att_own, att_other = chip_pair(att_matrix)
    core = lax.axis_index("ec")
    att_first = jnp.where(core == 0, att_own, att_other)
    att_second = jnp.where(core == 0, att_other, att_own)

    att_weight = pair_weights(att_logits, att_routes)
    att_place = slot_matrix(att_routes, capacity, EXPERTS)
    outgoing = jnp.dot(
        att_place.astype(jnp.bfloat16),
        context.reshape(-1, att_dim),
        preferred_element_type=jnp.float32,
    ).astype(jnp.bfloat16)
    incoming = dispatch(outgoing.reshape(capacity, EXPERTS, att_dim))
    rows_in = incoming.reshape(-1, att_dim)
    mapped = jnp.stack(
        [
            jnp.dot(rows_in, att_first, preferred_element_type=jnp.float32),
            jnp.dot(rows_in, att_second, preferred_element_type=jnp.float32),
        ],
        axis=1,
    ).astype(jnp.bfloat16)
    pair_width = CORES * out_slice
    mapped = mapped.reshape(n_ey, capacity, n_ez, pair_width)
    me = lax.axis_index("ey")
    twice = jnp.concatenate([mapped, mapped], axis=0)
    mapped = lax.dynamic_slice_in_dim(twice, (n_ey - me) % n_ey, n_ey, axis=0)
    mapped = jnp.transpose(mapped, (2, 0, 1, 3)).reshape(n_ez * n_ey, capacity, pair_width)
    back = lax.all_to_all(mapped, ("ez", "ey"), split_axis=0, concat_axis=0, tiled=True)
    back = back.reshape(EXPERTS, n_ey, capacity, pair_width)
    back = jnp.transpose(back, (2, 0, 1, 3)).reshape(capacity * EXPERTS, model_width)
    picked = jnp.dot(
        att_place.T.astype(jnp.bfloat16), back, preferred_element_type=jnp.float32
    )
    gate_matrix, _ = lax.optimization_barrier((gate_matrix, picked))
    depth = gate_matrix.shape[0]
    gate_own, gate_other = chip_pair(gate_matrix.reshape(depth, 2 * hid_slice))
    picked = picked.reshape(rows_dev, 2, model_width)
    hidden_state = (
        hidden_in.astype(jnp.float32)
        + att_weight[:, 0:1] * picked[:, 0]
        + att_weight[:, 1:2] * picked[:, 1]
    )
    ffn_in = norm_rows(hidden_state, norm_gain).astype(jnp.bfloat16)
    ffn_place = slot_matrix(ffn_routes, capacity, EXPERTS)
    row_place = jnp.any(ffn_place.reshape(EXPERTS * capacity, rows_dev, 2), axis=2)
    outgoing_rows = jnp.dot(
        row_place.astype(jnp.bfloat16), ffn_in, preferred_element_type=jnp.float32
    ).astype(jnp.bfloat16)
    arrived = lax.all_to_all(
        outgoing_rows.reshape(capacity, EXPERTS, model_width),
        "ez",
        split_axis=1,
        concat_axis=1,
        tiled=True,
    )
    own, right, far, left = ring_blocks(arrived)
    near = jnp.stack([own, right, left], axis=0).reshape(-1, model_width)
    far = far.reshape(-1, model_width)
    down_matrix, _ = lax.optimization_barrier((down_matrix, far))
    down_own, down_other = chip_pair(down_matrix)

    def slice_part(rows, gate_w, down_w):
        gate_up = jnp.dot(rows, gate_w, preferred_element_type=jnp.float32)
        gate_up = gate_up.reshape(-1, 2, hid_slice)
        activated = (jax.nn.silu(gate_up[:, 0]) * gate_up[:, 1]).astype(jnp.bfloat16)
        part = jnp.dot(activated, down_w, preferred_element_type=jnp.float32)
        return part.astype(jnp.bfloat16).astype(jnp.float32)

    far_part = slice_part(far, gate_own, down_own) + slice_part(far, gate_other, down_other)
    near_part = slice_part(near, gate_own, down_own) + slice_part(near, gate_other, down_other)
    near_part = near_part.reshape(3, -1, model_width)
    parts = [near_part[0], near_part[1], far_part, near_part[2]]
    reduced = ring_sums(parts).astype(jnp.bfloat16)
    reduced = reduced.reshape(capacity, n_ez, model_width)
    summed = lax.all_to_all(reduced, "ez", split_axis=1, concat_axis=1, tiled=True)
    summed = summed.reshape(capacity * EXPERTS, model_width).astype(jnp.float32)
    ffn_weight = pair_weights(ffn_logits, ffn_routes)
    weighted = ffn_place.astype(jnp.float32) * ffn_weight.reshape(1, -1)
    expert_mix = jnp.dot(weighted.T, summed, precision=lax.Precision.HIGHEST).reshape(
        rows_dev, 2, model_width
    )
    mixed_sum = hidden_state + (expert_mix[:, 0] + expert_mix[:, 1])
    return norm_rows(mixed_sum, out_gain).astype(jnp.bfloat16)


def solution(mesh):
    n_dp = mesh.devices.shape[0]
    n_expert = mesh.devices.shape[1]
    n_ey = n_expert // (EXPERTS * CORES)
    grid = Mesh(
        mesh.devices.reshape(n_dp, EXPERTS, n_ey, CORES), ("dp", "ez", "ey", "ec")
    )
    rows = ("dp", "ez", "ey", "ec")
    owners = ("ez", "ey", "ec")
    return jax.shard_map(
        local,
        mesh=grid,
        in_specs=(
            P(rows, None),
            P(rows, None, None),
            P(rows, None),
            P(rows, None),
            P(rows, None),
            P(rows, None),
            P(owners, "dp", None),
            P(owners, "dp", None, None),
            P(owners, None, "dp"),
            P(),
            P(),
        ),
        out_specs=P(rows, None),
        check_vma=False,
    )
```

```python
import jax
import jax.numpy as jnp
from jax import lax
from jax.sharding import Mesh
from jax.sharding import PartitionSpec as P

EXPERTS = 8
CAP = 20
CORES = 2


EPSILON = 1e-06


def norm_rows(values, gain):
    mean_square = jnp.mean(values * values, axis=-1, keepdims=True)
    return values * lax.rsqrt(mean_square + EPSILON) * gain.astype(jnp.float32)


def pair_weights(logits, routes):
    expert_ids = jnp.arange(logits.shape[1], dtype=jnp.int32)
    selected = routes[:, :, None] == expert_ids[None, None, :]
    chosen = jnp.sum(jnp.where(selected, logits[:, None, :], 0.0), axis=2)
    first_weight = jax.nn.sigmoid(chosen[:, 0] - chosen[:, 1])
    return jnp.stack([first_weight, 1.0 - first_weight], axis=1)


def slot_matrix(routes, capacity, experts):
    route_list = routes.reshape(-1)
    onehot = (route_list[:, None] == jnp.arange(experts, dtype=jnp.int32)[None, :]).astype(
        jnp.int32
    )
    before = jnp.cumsum(onehot, axis=0) - onehot
    slot_index = jnp.sum(before * onehot, axis=1)
    target = slot_index * experts + route_list
    slot_ids = jnp.arange(experts * capacity, dtype=jnp.int32)
    return slot_ids[:, None] == target[None, :]


def from_left(x):
    n = lax.axis_size("ey")
    return lax.ppermute(x, "ey", [(i, (i + 1) % n) for i in range(n)])


def from_right(x):
    n = lax.axis_size("ey")
    return lax.ppermute(x, "ey", [(i, (i - 1) % n) for i in range(n)])


def ring_copies(block):
    half = block.shape[0] // 2
    left = from_left(block)
    right = from_right(block)
    far = jnp.concatenate([from_left(left[:half]), from_right(right[half:])], axis=0)
    return jnp.stack([block, right, far, left], axis=0)


def ring_sums(parts):
    half = parts.shape[1] // 2
    far = parts[2].astype(jnp.bfloat16)
    early_right = from_right(far[:half]).astype(jnp.float32)
    early_left = from_left(far[half:]).astype(jnp.float32)
    to_left = jnp.concatenate([parts[3, :half] + early_right, parts[3, half:]], axis=0)
    to_right = jnp.concatenate([parts[1, :half], parts[1, half:] + early_left], axis=0)
    got_right = from_right(to_left.astype(jnp.bfloat16)).astype(jnp.float32)
    got_left = from_left(to_right.astype(jnp.bfloat16)).astype(jnp.float32)
    return parts[0] + got_right + got_left


def dispatch(blocks):
    arrived = lax.all_to_all(blocks, "ez", split_axis=1, concat_axis=1, tiled=True)
    return ring_copies(arrived)


def chip_pair(weights):
    return weights, lax.ppermute(weights, "ec", [(0, 1), (1, 0)])


def local(
    hidden_in,
    context,
    att_routes,
    att_logits,
    ffn_routes,
    ffn_logits,
    att_output_map,
    ffn_gate_up,
    ffn_down,
    norm_gain,
    out_gain,
):
    rows_dev = hidden_in.shape[0]
    model_width = hidden_in.shape[1]
    att_dim = context.shape[2]
    out_slice = att_output_map.shape[2]
    hid_slice = ffn_gate_up.shape[3]
    n_ez = lax.axis_size("ez")
    n_ey = lax.axis_size("ey")
    capacity = CAP

    att_matrix = lax.all_gather(att_output_map, "dp", axis=1, tiled=True)[0]
    gate_matrix = lax.all_gather(ffn_gate_up, "dp", axis=1, tiled=True)[0]
    down_matrix = lax.all_gather(ffn_down, "dp", axis=2, tiled=True)[0]
    att_own, att_other = chip_pair(att_matrix)
    core = lax.axis_index("ec")
    att_first = jnp.where(core == 0, att_own, att_other)
    att_second = jnp.where(core == 0, att_other, att_own)

    att_weight = pair_weights(att_logits, att_routes)
    att_place = slot_matrix(att_routes, capacity, EXPERTS)
    outgoing = jnp.dot(
        att_place.astype(jnp.bfloat16),
        context.reshape(-1, att_dim),
        preferred_element_type=jnp.float32,
    ).astype(jnp.bfloat16)
    incoming = dispatch(outgoing.reshape(capacity, EXPERTS, att_dim))
    rows_in = incoming.reshape(-1, att_dim)
    mapped = jnp.stack(
        [
            jnp.dot(rows_in, att_first, preferred_element_type=jnp.float32),
            jnp.dot(rows_in, att_second, preferred_element_type=jnp.float32),
        ],
        axis=1,
    ).astype(jnp.bfloat16)
    pair_width = CORES * out_slice
    mapped = mapped.reshape(n_ey, capacity, n_ez, pair_width)
    me = lax.axis_index("ey")
    twice = jnp.concatenate([mapped, mapped], axis=0)
    mapped = lax.dynamic_slice_in_dim(twice, (n_ey - me) % n_ey, n_ey, axis=0)
    mapped = jnp.transpose(mapped, (2, 0, 1, 3)).reshape(n_ez * n_ey, capacity, pair_width)
    back = lax.all_to_all(mapped, ("ez", "ey"), split_axis=0, concat_axis=0, tiled=True)
    back = back.reshape(EXPERTS, n_ey, capacity, pair_width)
    back = jnp.transpose(back, (2, 0, 1, 3)).reshape(capacity * EXPERTS, model_width)
    picked = jnp.dot(
        att_place.T.astype(jnp.bfloat16), back, preferred_element_type=jnp.float32
    )
    picked = picked.reshape(rows_dev, 2, model_width)
    hidden_state = (
        hidden_in.astype(jnp.float32)
        + att_weight[:, 0:1] * picked[:, 0]
        + att_weight[:, 1:2] * picked[:, 1]
    )
    ffn_in = norm_rows(hidden_state, norm_gain).astype(jnp.bfloat16)
    ffn_place = slot_matrix(ffn_routes, capacity, EXPERTS)
    row_place = jnp.any(ffn_place.reshape(EXPERTS * capacity, rows_dev, 2), axis=2)
    outgoing_rows = jnp.dot(
        row_place.astype(jnp.bfloat16), ffn_in, preferred_element_type=jnp.float32
    ).astype(jnp.bfloat16)
    arrived = lax.all_to_all(
        outgoing_rows.reshape(capacity, EXPERTS, model_width),
        "ez",
        split_axis=1,
        concat_axis=1,
        tiled=True,
    )
    gate_matrix, _ = lax.optimization_barrier((gate_matrix, arrived))
    depth = gate_matrix.shape[0]
    gate_own, gate_other = chip_pair(gate_matrix.reshape(depth, 2 * hid_slice))
    incoming = ring_copies(arrived)
    flattened = incoming.reshape(-1, model_width)
    down_matrix, _ = lax.optimization_barrier((down_matrix, incoming))
    down_own, down_other = chip_pair(down_matrix)

    def slice_part(gate_w, down_w):
        gate_up = jnp.dot(flattened, gate_w, preferred_element_type=jnp.float32)
        gate_up = gate_up.reshape(-1, 2, hid_slice)
        activated = (jax.nn.silu(gate_up[:, 0]) * gate_up[:, 1]).astype(jnp.bfloat16)
        part = jnp.dot(activated, down_w, preferred_element_type=jnp.float32)
        return part.astype(jnp.bfloat16).astype(jnp.float32)

    projected = slice_part(gate_own, down_own) + slice_part(gate_other, down_other)
    reduced = projected.reshape(n_ey, capacity * n_ez, model_width)
    reduced = ring_sums(reduced).astype(jnp.bfloat16)
    reduced = reduced.reshape(capacity, n_ez, model_width)
    summed = lax.all_to_all(reduced, "ez", split_axis=1, concat_axis=1, tiled=True)
    summed = summed.reshape(capacity * EXPERTS, model_width).astype(jnp.float32)
    ffn_weight = pair_weights(ffn_logits, ffn_routes)
    weighted = ffn_place.astype(jnp.float32) * ffn_weight.reshape(1, -1)
    expert_mix = jnp.dot(weighted.T, summed, precision=lax.Precision.HIGHEST).reshape(
        rows_dev, 2, model_width
    )
    mixed_sum = hidden_state + (expert_mix[:, 0] + expert_mix[:, 1])
    return norm_rows(mixed_sum, out_gain).astype(jnp.bfloat16)


def solution(mesh):
    n_dp = mesh.devices.shape[0]
    n_expert = mesh.devices.shape[1]
    n_ey = n_expert // (EXPERTS * CORES)
    grid = Mesh(
        mesh.devices.reshape(n_dp, EXPERTS, n_ey, CORES), ("dp", "ez", "ey", "ec")
    )
    rows = ("dp", "ez", "ey", "ec")
    owners = ("ez", "ey", "ec")
    return jax.shard_map(
        local,
        mesh=grid,
        in_specs=(
            P(rows, None),
            P(rows, None, None),
            P(rows, None),
            P(rows, None),
            P(rows, None),
            P(rows, None),
            P(owners, "dp", None),
            P(owners, "dp", None, None),
            P(owners, None, "dp"),
            P(),
            P(),
        ),
        out_specs=P(rows, None),
        check_vma=False,
    )
```

```python
import jax
import jax.numpy as jnp
from jax import lax
from jax.sharding import Mesh
from jax.sharding import PartitionSpec as P

EXPERTS = 8
CAP = 20
CORES = 2


EPSILON = 1e-06


def norm_rows(values, gain):
    mean_square = jnp.mean(values * values, axis=-1, keepdims=True)
    return values * lax.rsqrt(mean_square + EPSILON) * gain.astype(jnp.float32)


def pair_weights(logits, routes):
    expert_ids = jnp.arange(logits.shape[1], dtype=jnp.int32)
    selected = routes[:, :, None] == expert_ids[None, None, :]
    chosen = jnp.sum(jnp.where(selected, logits[:, None, :], 0.0), axis=2)
    first_weight = jax.nn.sigmoid(chosen[:, 0] - chosen[:, 1])
    return jnp.stack([first_weight, 1.0 - first_weight], axis=1)


def slot_matrix(routes, capacity, experts):
    route_list = routes.reshape(-1)
    onehot = (route_list[:, None] == jnp.arange(experts, dtype=jnp.int32)[None, :]).astype(
        jnp.int32
    )
    before = jnp.cumsum(onehot, axis=0) - onehot
    slot_index = jnp.sum(before * onehot, axis=1)
    target = slot_index * experts + route_list
    slot_ids = jnp.arange(experts * capacity, dtype=jnp.int32)
    return slot_ids[:, None] == target[None, :]


def from_left(x):
    n = lax.axis_size("ey")
    return lax.ppermute(x, "ey", [(i, (i + 1) % n) for i in range(n)])


def from_right(x):
    n = lax.axis_size("ey")
    return lax.ppermute(x, "ey", [(i, (i - 1) % n) for i in range(n)])


def ring_copies(block):
    half = block.shape[0] // 2
    left = from_left(block)
    right = from_right(block)
    far = jnp.concatenate([from_left(left[:half]), from_right(right[half:])], axis=0)
    return jnp.stack([block, right, far, left], axis=0)


def ring_sums(parts):
    half = parts.shape[1] // 2
    far = parts[2].astype(jnp.bfloat16)
    early_right = from_right(far[:half]).astype(jnp.float32)
    early_left = from_left(far[half:]).astype(jnp.float32)
    to_left = jnp.concatenate([parts[3, :half] + early_right, parts[3, half:]], axis=0)
    to_right = jnp.concatenate([parts[1, :half], parts[1, half:] + early_left], axis=0)
    got_right = from_right(to_left.astype(jnp.bfloat16)).astype(jnp.float32)
    got_left = from_left(to_right.astype(jnp.bfloat16)).astype(jnp.float32)
    return parts[0] + got_right + got_left


def dispatch(blocks):
    arrived = lax.all_to_all(blocks, "ez", split_axis=1, concat_axis=1, tiled=True)
    return ring_copies(arrived)


def chip_pair(weights):
    return weights, lax.ppermute(weights, "ec", [(0, 1), (1, 0)])


def local(
    hidden_in,
    context,
    att_routes,
    att_logits,
    ffn_routes,
    ffn_logits,
    att_output_map,
    ffn_gate_up,
    ffn_down,
    norm_gain,
    out_gain,
):
    rows_dev = hidden_in.shape[0]
    model_width = hidden_in.shape[1]
    att_dim = context.shape[2]
    out_slice = att_output_map.shape[2]
    hid_slice = ffn_gate_up.shape[3]
    n_ez = lax.axis_size("ez")
    n_ey = lax.axis_size("ey")
    capacity = CAP

    att_matrix = lax.all_gather(att_output_map, "dp", axis=1, tiled=True)[0]
    gate_matrix = lax.all_gather(ffn_gate_up, "dp", axis=1, tiled=True)[0]
    down_matrix = lax.all_gather(ffn_down, "dp", axis=2, tiled=True)[0]
    att_own, att_other = chip_pair(att_matrix)
    core = lax.axis_index("ec")
    att_first = jnp.where(core == 0, att_own, att_other)
    att_second = jnp.where(core == 0, att_other, att_own)

    att_weight = pair_weights(att_logits, att_routes)
    att_place = slot_matrix(att_routes, capacity, EXPERTS)
    outgoing = jnp.dot(
        att_place.astype(jnp.bfloat16),
        context.reshape(-1, att_dim),
        preferred_element_type=jnp.float32,
    ).astype(jnp.bfloat16)
    incoming = dispatch(outgoing.reshape(capacity, EXPERTS, att_dim))
    rows_in = incoming.reshape(-1, att_dim)
    mapped = jnp.stack(
        [
            jnp.dot(rows_in, att_first, preferred_element_type=jnp.float32),
            jnp.dot(rows_in, att_second, preferred_element_type=jnp.float32),
        ],
        axis=1,
    ).astype(jnp.bfloat16)
    pair_width = CORES * out_slice
    mapped = mapped.reshape(n_ey, capacity, n_ez, pair_width)
    me = lax.axis_index("ey")
    twice = jnp.concatenate([mapped, mapped], axis=0)
    mapped = lax.dynamic_slice_in_dim(twice, (n_ey - me) % n_ey, n_ey, axis=0)
    mapped = jnp.transpose(mapped, (2, 0, 1, 3)).reshape(n_ez * n_ey, capacity, pair_width)
    back = lax.all_to_all(mapped, ("ez", "ey"), split_axis=0, concat_axis=0, tiled=True)
    back = back.reshape(EXPERTS, n_ey, capacity, pair_width)
    back = jnp.transpose(back, (2, 0, 1, 3)).reshape(capacity * EXPERTS, model_width)
    picked = jnp.dot(
        att_place.T.astype(jnp.bfloat16), back, preferred_element_type=jnp.float32
    )
    picked = picked.reshape(rows_dev, 2, model_width)
    hidden_state = (
        hidden_in.astype(jnp.float32)
        + att_weight[:, 0:1] * picked[:, 0]
        + att_weight[:, 1:2] * picked[:, 1]
    )
    ffn_in = norm_rows(hidden_state, norm_gain).astype(jnp.bfloat16)
    ffn_place = slot_matrix(ffn_routes, capacity, EXPERTS)
    row_place = jnp.any(ffn_place.reshape(EXPERTS * capacity, rows_dev, 2), axis=2)
    outgoing_rows = jnp.dot(
        row_place.astype(jnp.bfloat16), ffn_in, preferred_element_type=jnp.float32
    ).astype(jnp.bfloat16)
    arrived = lax.all_to_all(
        outgoing_rows.reshape(capacity, EXPERTS, model_width),
        "ez",
        split_axis=1,
        concat_axis=1,
        tiled=True,
    )
    half = capacity // 2
    left = from_left(arrived)
    right = from_right(arrived)
    gate_matrix, _, _ = lax.optimization_barrier((gate_matrix, left, right))
    depth = gate_matrix.shape[0]
    gate_own, gate_other = chip_pair(gate_matrix.reshape(depth, 2 * hid_slice))
    far = jnp.concatenate([from_left(left[:half]), from_right(right[half:])], axis=0)
    incoming = jnp.stack([arrived, right, far, left], axis=0)
    flattened = incoming.reshape(-1, model_width)
    down_matrix, _ = lax.optimization_barrier((down_matrix, incoming))
    down_own, down_other = chip_pair(down_matrix)

    def slice_part(gate_w, down_w):
        gate_up = jnp.dot(flattened, gate_w, preferred_element_type=jnp.float32)
        gate_up = gate_up.reshape(-1, 2, hid_slice)
        activated = (jax.nn.silu(gate_up[:, 0]) * gate_up[:, 1]).astype(jnp.bfloat16)
        part = jnp.dot(activated, down_w, preferred_element_type=jnp.float32)
        return part.astype(jnp.bfloat16).astype(jnp.float32)

    projected = slice_part(gate_own, down_own) + slice_part(gate_other, down_other)
    reduced = projected.reshape(n_ey, capacity * n_ez, model_width)
    reduced = ring_sums(reduced).astype(jnp.bfloat16)
    reduced = reduced.reshape(capacity, n_ez, model_width)
    summed = lax.all_to_all(reduced, "ez", split_axis=1, concat_axis=1, tiled=True)
    summed = summed.reshape(capacity * EXPERTS, model_width).astype(jnp.float32)
    ffn_weight = pair_weights(ffn_logits, ffn_routes)
    weighted = ffn_place.astype(jnp.float32) * ffn_weight.reshape(1, -1)
    expert_mix = jnp.dot(weighted.T, summed, precision=lax.Precision.HIGHEST).reshape(
        rows_dev, 2, model_width
    )
    mixed_sum = hidden_state + (expert_mix[:, 0] + expert_mix[:, 1])
    return norm_rows(mixed_sum, out_gain).astype(jnp.bfloat16)


def solution(mesh):
    n_dp = mesh.devices.shape[0]
    n_expert = mesh.devices.shape[1]
    n_ey = n_expert // (EXPERTS * CORES)
    grid = Mesh(
        mesh.devices.reshape(n_dp, EXPERTS, n_ey, CORES), ("dp", "ez", "ey", "ec")
    )
    rows = ("dp", "ez", "ey", "ec")
    owners = ("ez", "ey", "ec")
    return jax.shard_map(
        local,
        mesh=grid,
        in_specs=(
            P(rows, None),
            P(rows, None, None),
            P(rows, None),
            P(rows, None),
            P(rows, None),
            P(rows, None),
            P(owners, "dp", None),
            P(owners, "dp", None, None),
            P(owners, None, "dp"),
            P(),
            P(),
        ),
        out_specs=P(rows, None),
        check_vma=False,
    )
```
